512 devices in a mesh: ctx: 64 (over y_lo, z, core), tp: 8 (over y_hi, x).
Axes of the slice: x: 4, y: 8 (y_hi: 2, y_lo: 4; y = y_hi * 4 + y_lo), z: 8, core: 2. Of those that a mesh axis runs over, the one named last changes fastest.
Arguments:
- tokens: bfloat16 [16384, 2048], P('ctx', 'tp'), may hold values from -6 to 6
- w_in: bfloat16 [2048, 4096], P('ctx', 'tp'), may hold values from -0.125 to 0.125
- w_bc: bfloat16 [2048, 2048], P('ctx', 'tp'), may hold values from -0.01171875 to 0.01171875
- w_dt: bfloat16 [2048, 64], P('ctx', 'tp'), may hold values from -0.125 to 0.125
- dt_bias: float32 [64], P('tp'), may hold values from -2 to 0
- decay_rate: float32 [64], P('tp'), may hold values from 1e-05 to 0.1
- skip_gain: float32 [64], P('tp'), may hold values from 0.5 to 1.5
- w_out: bfloat16 [4096, 2048], P('tp', 'ctx'), may hold values from -0.09375 to 0.09375
- cotangent: bfloat16 [16384, 2048], P('ctx', 'tp'), may hold values from -6 to 6
Outputs:
- output: bfloat16 [16384, 2048], P('ctx', 'tp')
- grad: bfloat16 [16384, 2048], P('ctx', 'tp')
The draws below stay inside these ranges and needn't reach their ends.
All inputs are finite; a program needn't handle non-finite values.
Results may differ from the reference program's by a relative error of at most 0.0061.
Values may be sent and summed in bfloat16 or wider, within the bound.
No kernel may reach another device: no remote copies, remote signals or barrier semaphores. Data moves between devices by JAX's collectives and lax.ppermute only.
A program may use at most 128 MiB of HBM per device.

```python
import math
import jax
import jax.numpy as jnp
from jax import lax

D = 2048
HEADS = 64
HEADDIM = 64
STATE = 128
GROUPS = 8
SPAN = 256
TOKENS = 16384
INNER = 4096


def levels(stream_key, dims, shards, least, high):
    gain = 1.0
    for dim, shards_of in shards:
        steps = jax.random.uniform(jax.random.fold_in(jax.random.fold_in(stream_key, 6), dim), (shards_of,), jnp.float32, least / len(shards), high / len(shards))
        gain = gain * jnp.repeat(jnp.exp(steps), dims[dim] // shards_of).reshape((-1,) + (1,) * (len(dims) - 1 - dim))
    return gain


def centred(key, extent, width, most, cuts=(), kind=jnp.bfloat16):
    entries = jax.random.normal(key, extent, jnp.float32) * width
    if len(cuts) > 0:
        entries = levels(key, extent, cuts, -0.22, 0.18) * entries
    return jnp.clip(entries, min=-most, max=most).astype(kind)


def setup_inputs(seed: int = 0) -> dict:
    arg_keys = jax.random.split(jax.random.key(seed), 10)
    tokens = centred(arg_keys[0], (TOKENS, D), 1.0, 6.0, ((0, 64), (1, 8)))
    w_in = centred(arg_keys[1], (D, INNER), D ** -0.5, 0.125, ((0, 64), (1, 8)))
    w_bc = centred(arg_keys[2], (D, GROUPS * 2 * STATE), (D * STATE) ** -0.5, 0.01171875, ((0, 64), (1, 8)))
    w_dt = centred(arg_keys[3], (D, HEADS), D ** -0.5, 0.125, ((0, 64), (1, 8)))
    dt_bias = jnp.clip(-2.0 + 2.0 * jax.random.uniform(arg_keys[4], (HEADS,), jnp.float32) ** levels(arg_keys[4], (HEADS,), ((0, 8),), -0.2, 0.2), -2.0, 0.0)
    decay_rate = jnp.clip(jnp.exp(math.log(0.1) - 9.2103404 * jax.random.uniform(arg_keys[5], (HEADS,), jnp.float32) ** levels(arg_keys[5], (HEADS,), ((0, 8),), -0.2, 0.2)), 9.999999747378752e-06, 0.1)
    skip_gain = jnp.clip(0.5 + 1.0 * jax.random.uniform(arg_keys[6], (HEADS,), jnp.float32) ** levels(arg_keys[6], (HEADS,), ((0, 8),), -0.2, 0.2), 0.5, 1.5)
    w_out = centred(arg_keys[7], (INNER, D), INNER ** -0.5, 0.09375, ((0, 8), (1, 64)))
    cotangent = centred(arg_keys[8], (TOKENS, D), 1.0, 6.0, ((0, 64), (1, 8)))
    return {"tokens": tokens, "w_in": w_in, "w_bc": w_bc, "w_dt": w_dt, "dt_bias": dt_bias, "decay_rate": decay_rate, "skip_gain": skip_gain, "w_out": w_out, "cotangent": cotangent}


HIGH = lax.Precision.HIGHEST

def ssd_core(values, b_rows, c_rows, step_size, decay_rate, state):
    length, heads, head_dim = values.shape
    groups = b_rows.shape[1]
    per_group = heads // groups
    blocks = length // SPAN
    lower_mask = (jnp.arange(SPAN)[:, None] >= jnp.arange(SPAN)[None, :])[None]

    def blocked(array):
        return array.reshape((blocks, SPAN) + array.shape[1:])

    def advance(carry, item):
        value_blk, b_blk, c_blk, step_blk = item
        cums = jnp.cumsum(-step_blk * decay_rate[None, :], axis=0)
        diff = cums.T[:, :, None] - cums.T[:, None, :]
        weight = jnp.where(lower_mask, jnp.exp(jnp.where(lower_mask, diff, 0.0)), 0.0)
        scores = jnp.einsum('tgn,sgn->gts', c_blk, b_blk, precision=HIGH)
        scores = jnp.repeat(scores, per_group, axis=0)
        inputs = step_blk[:, :, None] * value_blk
        inside = jnp.einsum('hts,shp->thp', scores * weight, inputs, precision=HIGH)
        c_head = jnp.repeat(c_blk, per_group, axis=1)
        b_head = jnp.repeat(b_blk, per_group, axis=1)
        carried = jnp.exp(cums)[:, :, None] * jnp.einsum('thn,hpn->thp', c_head, carry, precision=HIGH)
        tail = jnp.exp(cums[-1][None, :] - cums)
        fresh = jnp.einsum('shp,shn->hpn', tail[:, :, None] * inputs, b_head, precision=HIGH)
        carry = jnp.exp(cums[-1])[:, None, None] * carry + fresh
        return (carry, inside + carried)
    final, outputs = lax.scan(jax.checkpoint(advance), state, (blocked(values), blocked(b_rows), blocked(c_rows), blocked(step_size)))
    return (outputs.reshape(length, heads, head_dim), final)

def reference(tokens, w_in, w_bc, w_dt, dt_bias, decay_rate, skip_gain, w_out, cotangent):
    total = tokens.shape[0]
    heads = decay_rate.shape[0]
    inner = w_in.shape[1]
    groups = w_bc.shape[1] // (2 * STATE)
    values = jnp.dot(tokens, w_in, preferred_element_type=jnp.float32).astype(jnp.bfloat16)
    pairs = jnp.dot(tokens, w_bc, preferred_element_type=jnp.float32).astype(jnp.bfloat16)
    pre_step = jnp.dot(tokens, w_dt, preferred_element_type=jnp.float32) + dt_bias[None, :]
    step_size = jax.nn.softplus(pre_step)
    value_f = values.astype(jnp.float32).reshape(total, heads, HEADDIM)
    paired = pairs.astype(jnp.float32).reshape(total, groups, 2, STATE)
    b_rows = paired[:, :, 0]
    c_rows = paired[:, :, 1]
    zero_state = jnp.zeros((heads, HEADDIM, STATE), jnp.float32)

    def scan_only(vals, brows, crows, steps):
        return ssd_core(vals, brows, crows, steps, decay_rate, zero_state)[0]
    core_out, pullback = jax.vjp(scan_only, value_f, b_rows, c_rows, step_size)
    mixed = (core_out + skip_gain[None, :, None] * value_f).reshape(total, inner).astype(jnp.bfloat16)
    output = jnp.dot(mixed, w_out, preferred_element_type=jnp.float32).astype(jnp.bfloat16)
    d_mixed = jnp.dot(cotangent, w_out.T, preferred_element_type=jnp.float32).reshape(total, heads, HEADDIM)
    d_values, d_brows, d_crows, d_step = pullback(d_mixed)
    d_values = d_values + skip_gain[None, :, None] * d_mixed
    d_pre = d_step * jax.nn.sigmoid(pre_step)
    d_pairs = jnp.stack([d_brows, d_crows], axis=2).reshape(total, groups * 2 * STATE)
    grad = jnp.dot(d_values.reshape(total, inner).astype(jnp.bfloat16), w_in.T, preferred_element_type=jnp.float32)
    grad = grad + jnp.dot(d_pairs.astype(jnp.bfloat16), w_bc.T, preferred_element_type=jnp.float32)
    grad = grad + jnp.dot(d_pre.astype(jnp.bfloat16), w_dt.T, preferred_element_type=jnp.float32)
    return (output, grad.astype(jnp.bfloat16))
```

```python
import jax
import jax.numpy as jnp
from jax import lax
from jax.sharding import PartitionSpec as P

HEADDIM = 64
STATE = 128
SPAN = 256


HIGH = lax.Precision.HIGHEST


def carried_in(decay, state, axis, reverse):
    devices, position = (lax.axis_size(axis), lax.axis_index(axis))
    heads = decay.shape[0]
    packed = jnp.concatenate(
        [state.reshape(heads, -1), jnp.broadcast_to(decay[:, None], (heads, 128))], axis=1
    )

    def shifted(x, shift):
        if reverse:
            perm = [(i + shift, i) for i in range(devices - shift)]
        else:
            perm = [(i, i + shift) for i in range(devices - shift)]
        return lax.ppermute(x, axis, perm)

    shift = 1
    while shift < devices:
        got = shifted(packed, shift)
        own = packed[:, -128:]
        reached = position < devices - shift if reverse else position >= shift
        mixed_s = own[:, :1] * got[:, :-128] + packed[:, :-128]
        mixed_a = jnp.where(reached, own * got[:, -128:], own)
        packed = jnp.concatenate([mixed_s, mixed_a], axis=1)
        shift *= 2
    before = shifted(packed[:, :-128], 1)
    return before.reshape(state.shape)


def ssd_core(values, b_rows, c_rows, step_size, decay_rate, state):
    length, heads, head_dim = values.shape
    groups = b_rows.shape[1]
    per_group = heads // groups
    blocks = length // SPAN
    lower_mask = (jnp.arange(SPAN)[:, None] >= jnp.arange(SPAN)[None, :])[None]

    def blocked(array):
        return array.reshape((blocks, SPAN) + array.shape[1:])

    def ssd_advance(carry, item):
        value_blk, b_blk, c_blk, step_blk = item
        cums = jnp.cumsum(-step_blk * decay_rate[None, :], axis=0)
        diff = cums.T[:, :, None] - cums.T[:, None, :]
        weight = jnp.where(lower_mask, jnp.exp(jnp.where(lower_mask, diff, 0.0)), 0.0)
        scores = jnp.einsum("tgn,sgn->gts", c_blk, b_blk, precision=HIGH)
        scores = jnp.repeat(scores, per_group, axis=0)
        inputs = step_blk[:, :, None] * value_blk
        inside = jnp.einsum("hts,shp->thp", scores * weight, inputs, precision=HIGH)
        c_head = jnp.repeat(c_blk, per_group, axis=1)
        b_head = jnp.repeat(b_blk, per_group, axis=1)
        carried = jnp.exp(cums)[:, :, None] * jnp.einsum(
            "thn,hpn->thp", c_head, carry, precision=HIGH
        )
        tail = jnp.exp(cums[-1][None, :] - cums)
        fresh = jnp.einsum("shp,shn->hpn", tail[:, :, None] * inputs, b_head, precision=HIGH)
        carry = jnp.exp(cums[-1])[:, None, None] * carry + fresh
        return (carry, inside + carried)

    final, outputs = lax.scan(
        jax.checkpoint(ssd_advance),
        state,
        (blocked(values), blocked(b_rows), blocked(c_rows), blocked(step_size)),
    )
    return (outputs.reshape(length, heads, head_dim), final)


def local_states(values, b_rows, step_size, decay_rate):
    length, heads, head_dim = values.shape
    groups = b_rows.shape[1]
    per_group = heads // groups
    blocks = length // SPAN

    def blocked(array):
        return array.reshape((blocks, SPAN) + array.shape[1:])

    def local_advance(carry, item):
        value_blk, b_blk, step_blk = item
        cums = jnp.cumsum(-step_blk * decay_rate[None, :], axis=0)
        tail = jnp.exp(cums[-1][None, :] - cums)
        b_head = jnp.repeat(b_blk, per_group, axis=1)
        inputs = (tail * step_blk)[:, :, None] * value_blk
        fresh = jnp.einsum("shp,shn->hpn", inputs, b_head, precision=HIGH)
        return (jnp.exp(cums[-1])[:, None, None] * carry + fresh, None)

    start = jnp.zeros((heads, head_dim, STATE), jnp.float32)
    final, unused = lax.scan(
        local_advance, start, (blocked(values), blocked(b_rows), blocked(step_size))
    )
    return final


def local_adjoint(d_mixed, c_rows, step_size, decay_rate):
    length, heads, head_dim = d_mixed.shape
    groups = c_rows.shape[1]
    per_group = heads // groups
    blocks = length // SPAN

    def blocked(array):
        return array.reshape((blocks, SPAN) + array.shape[1:])

    def retreat(carry, item):
        grad_blk, c_blk, step_blk = item
        cums = jnp.cumsum(-step_blk * decay_rate[None, :], axis=0)
        c_head = jnp.repeat(c_blk, per_group, axis=1)
        weighted = jnp.exp(cums)[:, :, None] * grad_blk
        term = jnp.einsum("thp,thn->hpn", weighted, c_head, precision=HIGH)
        return (term + jnp.exp(cums[-1])[:, None, None] * carry, None)

    start = jnp.zeros((heads, head_dim, STATE), jnp.float32)
    final, unused = lax.scan(
        retreat, start, (blocked(d_mixed), blocked(c_rows), blocked(step_size)), reverse=True
    )
    return final


def per_device(tokens, w_in, w_bc, w_dt, dt_bias, decay_rate, skip_gain, w_out, cotangent):
    full_tokens = lax.all_gather(tokens, "tp", axis=1, tiled=True)
    rows = full_tokens.shape[0]
    heads = decay_rate.shape[0]
    inner = w_in.shape[1]
    pair_cols = w_bc.shape[1]
    groups = pair_cols // (2 * STATE)
    w_cat = jnp.concatenate([w_in, w_bc, w_dt], axis=1)
    whole_in, whole_out = (
        lax.all_gather(w_cat, "ctx", axis=0, tiled=True),
        lax.all_gather(w_out, "ctx", axis=1, tiled=True),
    )
    projected = jnp.dot(full_tokens, whole_in, preferred_element_type=jnp.float32)
    values = projected[:, :inner].astype(jnp.bfloat16)
    pairs = projected[:, inner : inner + pair_cols].astype(jnp.bfloat16)
    pre_step = projected[:, inner + pair_cols :] + dt_bias[None, :]
    step_size = jax.nn.softplus(pre_step)
    value_f = values.astype(jnp.float32).reshape(rows, heads, HEADDIM)
    paired = pairs.astype(jnp.float32).reshape(rows, groups, 2, STATE)
    b_rows = paired[:, :, 0]
    c_rows = paired[:, :, 1]
    zero_state = jnp.zeros((heads, HEADDIM, STATE), jnp.float32)
    end_state = local_states(value_f, b_rows, step_size, decay_rate)
    decay_total = jnp.exp(-jnp.sum(step_size * decay_rate[None, :], axis=0))
    state_in = carried_in(decay_total, end_state, "ctx", False)

    def with_state(vals, brows, crows, steps):
        return ssd_core(vals, brows, crows, steps, decay_rate, state_in)

    (core_out, core_end), pullback = jax.vjp(with_state, value_f, b_rows, c_rows, step_size)
    mixed = (
        (core_out + skip_gain[None, :, None] * value_f).reshape(rows, inner).astype(jnp.bfloat16)
    )
    partial_out = jnp.dot(mixed, whole_out, preferred_element_type=jnp.float32)
    output = lax.psum_scatter(partial_out, "tp", scatter_dimension=1, tiled=True).astype(
        jnp.bfloat16
    )
    full_cotangent = lax.all_gather(cotangent, "tp", axis=1, tiled=True)
    d_flat = lax.dot_general(
        full_cotangent, whole_out, (((1,), (1,)), ((), ())), preferred_element_type=jnp.float32
    )
    d_mixed = d_flat.reshape(rows, heads, HEADDIM)
    own_adjoint = local_adjoint(d_mixed, c_rows, step_size, decay_rate)
    adjoint = carried_in(decay_total, own_adjoint, "ctx", True)
    grads = pullback((d_mixed, adjoint))
    d_values = grads[0] + skip_gain[None, :, None] * d_mixed
    d_pre = grads[3] * jax.nn.sigmoid(pre_step)
    d_pairs = jnp.stack([grads[1], grads[2]], axis=2).reshape(rows, pair_cols)
    d_cat = jnp.concatenate(
        [
            d_values.reshape(rows, inner).astype(jnp.bfloat16),
            d_pairs.astype(jnp.bfloat16),
            d_pre.astype(jnp.bfloat16),
        ],
        axis=1,
    )
    partial_grad = lax.dot_general(
        d_cat, whole_in, (((1,), (1,)), ((), ())), preferred_element_type=jnp.float32
    )
    grad = lax.psum_scatter(partial_grad, "tp", scatter_dimension=1, tiled=True).astype(
        jnp.bfloat16
    )
    return (output, grad)


def solution(mesh):
    placed = (
        P("ctx", "tp"),
        P("ctx", "tp"),
        P("ctx", "tp"),
        P("ctx", "tp"),
        P("tp"),
        P("tp"),
        P("tp"),
        P("tp", "ctx"),
        P("ctx", "tp"),
    )
    return jax.shard_map(
        per_device,
        mesh=mesh,
        in_specs=placed,
        out_specs=(P("ctx", "tp"), P("ctx", "tp")),
        check_vma=False,
    )
```

```python
import jax
import jax.numpy as jnp
from jax import lax
from jax.sharding import PartitionSpec as P

HEADDIM = 64
STATE = 128
SPAN = 256


HIGH = lax.Precision.HIGHEST


def carried_in(decay, state, axis, reverse):
    devices, position = (lax.axis_size(axis), lax.axis_index(axis))
    heads = decay.shape[0]
    packed = jnp.concatenate(
        [state.reshape(heads, -1), jnp.broadcast_to(decay[:, None], (heads, 128))], axis=1
    )

    def shifted(x, shift):
        if reverse:
            perm = [(i + shift, i) for i in range(devices - shift)]
        else:
            perm = [(i, i + shift) for i in range(devices - shift)]
        return lax.ppermute(x, axis, perm)

    shift = 1
    while shift < devices:
        got = shifted(packed, shift)
        own = packed[:, -128:]
        reached = position < devices - shift if reverse else position >= shift
        mixed_s = own[:, :1] * got[:, :-128] + packed[:, :-128]
        mixed_a = jnp.where(reached, own * got[:, -128:], own)
        packed = jnp.concatenate([mixed_s, mixed_a], axis=1)
        shift *= 2
    before = shifted(packed[:, :-128], 1)
    return before.reshape(state.shape)


def ssd_core(values, b_rows, c_rows, step_size, decay_rate, state):
    length, heads, head_dim = values.shape
    groups = b_rows.shape[1]
    per_group = heads // groups
    blocks = length // SPAN
    lower_mask = (jnp.arange(SPAN)[:, None] >= jnp.arange(SPAN)[None, :])[None]

    def blocked(array):
        return array.reshape((blocks, SPAN) + array.shape[1:])

    def ssd_advance(carry, item):
        value_blk, b_blk, c_blk, step_blk = item
        cums = jnp.cumsum(-step_blk * decay_rate[None, :], axis=0)
        diff = cums.T[:, :, None] - cums.T[:, None, :]
        weight = jnp.where(lower_mask, jnp.exp(jnp.where(lower_mask, diff, 0.0)), 0.0)
        scores = jnp.einsum("tgn,sgn->gts", c_blk, b_blk, precision=HIGH)
        scores = jnp.repeat(scores, per_group, axis=0)
        inputs = step_blk[:, :, None] * value_blk
        inside = jnp.einsum("hts,shp->thp", scores * weight, inputs, precision=HIGH)
        c_head = jnp.repeat(c_blk, per_group, axis=1)
        b_head = jnp.repeat(b_blk, per_group, axis=1)
        carried = jnp.exp(cums)[:, :, None] * jnp.einsum(
            "thn,hpn->thp", c_head, carry, precision=HIGH
        )
        tail = jnp.exp(cums[-1][None, :] - cums)
        fresh = jnp.einsum("shp,shn->hpn", tail[:, :, None] * inputs, b_head, precision=HIGH)
        carry = jnp.exp(cums[-1])[:, None, None] * carry + fresh
        return (carry, inside + carried)

    final, outputs = lax.scan(
        jax.checkpoint(ssd_advance),
        state,
        (blocked(values), blocked(b_rows), blocked(c_rows), blocked(step_size)),
    )
    return (outputs.reshape(length, heads, head_dim), final)


def local_states(values, b_rows, step_size, decay_rate):
    length, heads, head_dim = values.shape
    groups = b_rows.shape[1]
    per_group = heads // groups
    blocks = length // SPAN

    def blocked(array):
        return array.reshape((blocks, SPAN) + array.shape[1:])

    def local_advance(carry, item):
        value_blk, b_blk, step_blk = item
        cums = jnp.cumsum(-step_blk * decay_rate[None, :], axis=0)
        tail = jnp.exp(cums[-1][None, :] - cums)
        b_head = jnp.repeat(b_blk, per_group, axis=1)
        inputs = (tail * step_blk)[:, :, None] * value_blk
        fresh = jnp.einsum("shp,shn->hpn", inputs, b_head, precision=HIGH)
        return (jnp.exp(cums[-1])[:, None, None] * carry + fresh, None)

    start = jnp.zeros((heads, head_dim, STATE), jnp.float32)
    final, unused = lax.scan(
        local_advance, start, (blocked(values), blocked(b_rows), blocked(step_size))
    )
    return final


def local_adjoint(d_mixed, c_rows, step_size, decay_rate):
    length, heads, head_dim = d_mixed.shape
    groups = c_rows.shape[1]
    per_group = heads // groups
    blocks = length // SPAN

    def blocked(array):
        return array.reshape((blocks, SPAN) + array.shape[1:])

    def retreat(carry, item):
        grad_blk, c_blk, step_blk = item
        cums = jnp.cumsum(-step_blk * decay_rate[None, :], axis=0)
        c_head = jnp.repeat(c_blk, per_group, axis=1)
        weighted = jnp.exp(cums)[:, :, None] * grad_blk
        term = jnp.einsum("thp,thn->hpn", weighted, c_head, precision=HIGH)
        return (term + jnp.exp(cums[-1])[:, None, None] * carry, None)

    start = jnp.zeros((heads, head_dim, STATE), jnp.float32)
    final, unused = lax.scan(
        retreat, start, (blocked(d_mixed), blocked(c_rows), blocked(step_size)), reverse=True
    )
    return final


def from_each(x, axis):
    devices = lax.axis_size(axis)
    got = [x]
    for k in range(1, devices):
        got.append(lax.ppermute(x, axis, [(i, (i + k) % devices) for i in range(devices)]))
    return got


def summed_over(part_for, axis):
    devices, position = (lax.axis_size(axis), lax.axis_index(axis))
    total = part_for(position)
    for k in range(1, devices):
        part = part_for((position + k) % devices)
        total = total + lax.ppermute(
            part, axis, [(i, (i + k) % devices) for i in range(devices)]
        )
    return total


def row_block(w, index, size):
    return lax.dynamic_slice_in_dim(w, index * size, size, axis=0)


def per_device(tokens, w_in, w_bc, w_dt, dt_bias, decay_rate, skip_gain, w_out, cotangent):
    devices, position = (lax.axis_size("tp"), lax.axis_index("tp"))
    rows, width = tokens.shape
    heads = decay_rate.shape[0]
    inner = w_in.shape[1]
    pair_cols = w_bc.shape[1]
    groups = pair_cols // (2 * STATE)
    out_cols = w_out.shape[0]
    w_all = lax.all_gather(
        jnp.concatenate([w_out.T, w_in, w_bc, w_dt], axis=1), "ctx", axis=0, tiled=True
    )
    pieces = from_each(jnp.concatenate([tokens, cotangent], axis=1), "tp")
    projected = None
    d_flat = None
    for k in range(devices):
        block = row_block(w_all, (position - k) % devices, width)
        term = jnp.dot(pieces[k][:, :width], block[:, out_cols:], preferred_element_type=jnp.float32)
        projected = term if projected is None else projected + term
        term = jnp.dot(pieces[k][:, width:], block[:, :out_cols], preferred_element_type=jnp.float32)
        d_flat = term if d_flat is None else d_flat + term
    values = projected[:, :inner].astype(jnp.bfloat16)
    pairs = projected[:, inner : inner + pair_cols].astype(jnp.bfloat16)
    pre_step = projected[:, inner + pair_cols :] + dt_bias[None, :]
    step_size = jax.nn.softplus(pre_step)
    value_f = values.astype(jnp.float32).reshape(rows, heads, HEADDIM)
    paired = pairs.astype(jnp.float32).reshape(rows, groups, 2, STATE)
    b_rows = paired[:, :, 0]
    c_rows = paired[:, :, 1]
    end_state = local_states(value_f, b_rows, step_size, decay_rate)
    decay_total = jnp.exp(-jnp.sum(step_size * decay_rate[None, :], axis=0))
    state_in = carried_in(decay_total, end_state, "ctx", False)

    def with_state(vals, brows, crows, steps):
        return ssd_core(vals, brows, crows, steps, decay_rate, state_in)

    (core_out, core_end), pullback = jax.vjp(with_state, value_f, b_rows, c_rows, step_size)
    mixed = (
        (core_out + skip_gain[None, :, None] * value_f).reshape(rows, inner).astype(jnp.bfloat16)
    )

    def out_part(dest):
        block = row_block(w_all, dest, width)[:, :out_cols]
        return lax.dot_general(
            mixed, block, (((1,), (1,)), ((), ())), preferred_element_type=jnp.float32
        )

    output = summed_over(out_part, "tp").astype(jnp.bfloat16)
    d_mixed = d_flat.reshape(rows, heads, HEADDIM)
    own_adjoint = local_adjoint(d_mixed, c_rows, step_size, decay_rate)
    adjoint = carried_in(decay_total, own_adjoint, "ctx", True)
    grads = pullback((d_mixed, adjoint))
    d_values = grads[0] + skip_gain[None, :, None] * d_mixed
    d_pre = grads[3] * jax.nn.sigmoid(pre_step)
    d_pairs = jnp.stack([grads[1], grads[2]], axis=2).reshape(rows, pair_cols)
    d_cat = jnp.concatenate(
        [
            d_values.reshape(rows, inner).astype(jnp.bfloat16),
            d_pairs.astype(jnp.bfloat16),
            d_pre.astype(jnp.bfloat16),
        ],
        axis=1,
    )

    def grad_part(dest):
        block = row_block(w_all, dest, width)[:, out_cols:]
        return lax.dot_general(
            d_cat, block, (((1,), (1,)), ((), ())), preferred_element_type=jnp.float32
        )

    grad = summed_over(grad_part, "tp").astype(jnp.bfloat16)
    return (output, grad)


def solution(mesh):
    placed = (
        P("ctx", "tp"),
        P("ctx", "tp"),
        P("ctx", "tp"),
        P("ctx", "tp"),
        P("tp"),
        P("tp"),
        P("tp"),
        P("tp", "ctx"),
        P("ctx", "tp"),
    )
    return jax.shard_map(
        per_device,
        mesh=mesh,
        in_specs=placed,
        out_specs=(P("ctx", "tp"), P("ctx", "tp")),
        check_vma=False,
    )
```

```python
import jax
import jax.numpy as jnp
from jax import lax
from jax.sharding import PartitionSpec as P

HEADDIM = 64
STATE = 128
SPAN = 256


HIGH = lax.Precision.HIGHEST


def both_carries(decay, forward, backward, axis):
    devices, position = (lax.axis_size(axis), lax.axis_index(axis))
    heads = decay.shape[0]
    total_a = decay[:, None]
    total_s = forward.reshape(heads, -1)
    total_u = backward.reshape(heads, -1)
    size = total_s.shape[1]
    before_a = jnp.ones_like(total_a)
    before_s = jnp.zeros_like(total_s)
    after_a = jnp.ones_like(total_a)
    after_u = jnp.zeros_like(total_u)
    bit = 1
    while bit < devices:
        message = jnp.concatenate(
            [total_s, total_u, jnp.broadcast_to(total_a, (heads, 128))], axis=1
        )
        got = lax.ppermute(message, axis, [(i, i ^ bit) for i in range(devices)])
        got_s = got[:, :size]
        got_u = got[:, size : 2 * size]
        got_a = got[:, 2 * size : 2 * size + 1]
        lower = (position & bit) != 0
        before_s = jnp.where(lower, before_a * got_s + before_s, before_s)
        before_a = jnp.where(lower, got_a * before_a, before_a)
        after_u = jnp.where(lower, after_u, after_u + after_a * got_u)
        after_a = jnp.where(lower, after_a, after_a * got_a)
        total_s = jnp.where(lower, total_a * got_s + total_s, got_a * total_s + got_s)
        total_u = jnp.where(lower, got_u + got_a * total_u, total_u + total_a * got_u)
        total_a = total_a * got_a
        bit *= 2
    return before_s.reshape(forward.shape), after_u.reshape(backward.shape)


def scattered_sum(partial, axis, width):
    devices, position = (lax.axis_size(axis), lax.axis_index(axis))
    rows = partial.shape[0]
    blocks = partial.reshape(rows, devices, width)
    bit = 1
    while bit < devices:
        count = blocks.shape[1]
        paired = blocks.reshape(rows, count // 2, 2, width)
        mine = (position & bit) != 0
        keep = jnp.where(mine, paired[:, :, 1], paired[:, :, 0])
        send = jnp.where(mine, paired[:, :, 0], paired[:, :, 1])
        blocks = keep + lax.ppermute(send, axis, [(i, i ^ bit) for i in range(devices)])
        bit *= 2
    return blocks.reshape(rows, width)


def ssd_core(values, b_rows, c_rows, step_size, decay_rate, state):
    length, heads, head_dim = values.shape
    groups = b_rows.shape[1]
    per_group = heads // groups
    blocks = length // SPAN
    lower_mask = (jnp.arange(SPAN)[:, None] >= jnp.arange(SPAN)[None, :])[None]

    def blocked(array):
        return array.reshape((blocks, SPAN) + array.shape[1:])

    def ssd_advance(carry, item):
        value_blk, b_blk, c_blk, step_blk = item
        cums = jnp.cumsum(-step_blk * decay_rate[None, :], axis=0)
        diff = cums.T[:, :, None] - cums.T[:, None, :]
        weight = jnp.where(lower_mask, jnp.exp(jnp.where(lower_mask, diff, 0.0)), 0.0)
        scores = jnp.einsum("tgn,sgn->gts", c_blk, b_blk, precision=HIGH)
        scores = jnp.repeat(scores, per_group, axis=0)
        inputs = step_blk[:, :, None] * value_blk
        inside = jnp.einsum("hts,shp->thp", scores * weight, inputs, precision=HIGH)
        c_head = jnp.repeat(c_blk, per_group, axis=1)
        b_head = jnp.repeat(b_blk, per_group, axis=1)
        carried = jnp.exp(cums)[:, :, None] * jnp.einsum(
            "thn,hpn->thp", c_head, carry, precision=HIGH
        )
        tail = jnp.exp(cums[-1][None, :] - cums)
        fresh = jnp.einsum("shp,shn->hpn", tail[:, :, None] * inputs, b_head, precision=HIGH)
        carry = jnp.exp(cums[-1])[:, None, None] * carry + fresh
        return (carry, inside + carried)

    final, outputs = lax.scan(
        jax.checkpoint(ssd_advance),
        state,
        (blocked(values), blocked(b_rows), blocked(c_rows), blocked(step_size)),
    )
    return (outputs.reshape(length, heads, head_dim), final)


def local_states(values, b_rows, step_size, decay_rate):
    length, heads, head_dim = values.shape
    groups = b_rows.shape[1]
    per_group = heads // groups
    blocks = length // SPAN

    def blocked(array):
        return array.reshape((blocks, SPAN) + array.shape[1:])

    def local_advance(carry, item):
        value_blk, b_blk, step_blk = item
        cums = jnp.cumsum(-step_blk * decay_rate[None, :], axis=0)
        tail = jnp.exp(cums[-1][None, :] - cums)
        b_head = jnp.repeat(b_blk, per_group, axis=1)
        inputs = (tail * step_blk)[:, :, None] * value_blk
        fresh = jnp.einsum("shp,shn->hpn", inputs, b_head, precision=HIGH)
        return (jnp.exp(cums[-1])[:, None, None] * carry + fresh, None)

    start = jnp.zeros((heads, head_dim, STATE), jnp.float32)
    final, unused = lax.scan(
        local_advance, start, (blocked(values), blocked(b_rows), blocked(step_size))
    )
    return final


def local_adjoint(d_mixed, c_rows, step_size, decay_rate):
    length, heads, head_dim = d_mixed.shape
    groups = c_rows.shape[1]
    per_group = heads // groups
    blocks = length // SPAN

    def blocked(array):
        return array.reshape((blocks, SPAN) + array.shape[1:])

    def retreat(carry, item):
        grad_blk, c_blk, step_blk = item
        cums = jnp.cumsum(-step_blk * decay_rate[None, :], axis=0)
        c_head = jnp.repeat(c_blk, per_group, axis=1)
        weighted = jnp.exp(cums)[:, :, None] * grad_blk
        term = jnp.einsum("thp,thn->hpn", weighted, c_head, precision=HIGH)
        return (term + jnp.exp(cums[-1])[:, None, None] * carry, None)

    start = jnp.zeros((heads, head_dim, STATE), jnp.float32)
    final, unused = lax.scan(
        retreat, start, (blocked(d_mixed), blocked(c_rows), blocked(step_size)), reverse=True
    )
    return final


def from_each(x, axis):
    devices = lax.axis_size(axis)
    got = [x]
    for k in range(1, devices):
        got.append(lax.ppermute(x, axis, [(i, (i + k) % devices) for i in range(devices)]))
    return got


def row_block(w, index, size):
    return lax.dynamic_slice_in_dim(w, index * size, size, axis=0)


def per_device(tokens, w_in, w_bc, w_dt, dt_bias, decay_rate, skip_gain, w_out, cotangent):
    devices, position = (lax.axis_size("tp"), lax.axis_index("tp"))
    rows, width = tokens.shape
    heads = decay_rate.shape[0]
    inner = w_in.shape[1]
    pair_cols = w_bc.shape[1]
    groups = pair_cols // (2 * STATE)
    out_cols = w_out.shape[0]
    w_all = lax.all_gather(
        jnp.concatenate([w_out.T, w_in, w_bc, w_dt], axis=1), "ctx", axis=0, tiled=True
    )
    pieces = from_each(jnp.concatenate([tokens, cotangent], axis=1), "tp")
    projected = None
    d_flat = None
    for k in range(devices):
        block = row_block(w_all, (position - k) % devices, width)
        term = jnp.dot(pieces[k][:, :width], block[:, out_cols:], preferred_element_type=jnp.float32)
        projected = term if projected is None else projected + term
        term = jnp.dot(pieces[k][:, width:], block[:, :out_cols], preferred_element_type=jnp.float32)
        d_flat = term if d_flat is None else d_flat + term
    values = projected[:, :inner].astype(jnp.bfloat16)
    pairs = projected[:, inner : inner + pair_cols].astype(jnp.bfloat16)
    pre_step = projected[:, inner + pair_cols :] + dt_bias[None, :]
    step_size = jax.nn.softplus(pre_step)
    value_f = values.astype(jnp.float32).reshape(rows, heads, HEADDIM)
    paired = pairs.astype(jnp.float32).reshape(rows, groups, 2, STATE)
    b_rows = paired[:, :, 0]
    c_rows = paired[:, :, 1]
    end_state = local_states(value_f, b_rows, step_size, decay_rate)
    decay_total = jnp.exp(-jnp.sum(step_size * decay_rate[None, :], axis=0))
    d_mixed = d_flat.reshape(rows, heads, HEADDIM)
    own_adjoint = local_adjoint(d_mixed, c_rows, step_size, decay_rate)
    state_in, adjoint = both_carries(decay_total, end_state, own_adjoint, "ctx")

    def with_state(vals, brows, crows, steps):
        return ssd_core(vals, brows, crows, steps, decay_rate, state_in)

    (core_out, core_end), pullback = jax.vjp(with_state, value_f, b_rows, c_rows, step_size)
    mixed = (
        (core_out + skip_gain[None, :, None] * value_f).reshape(rows, inner).astype(jnp.bfloat16)
    )

    partial_out = lax.dot_general(
        mixed, w_all[:, :out_cols], (((1,), (1,)), ((), ())), preferred_element_type=jnp.float32
    )
    output = scattered_sum(partial_out, "tp", width).astype(jnp.bfloat16)
    grads = pullback((d_mixed, adjoint))
    d_values = grads[0] + skip_gain[None, :, None] * d_mixed
    d_pre = grads[3] * jax.nn.sigmoid(pre_step)
    d_pairs = jnp.stack([grads[1], grads[2]], axis=2).reshape(rows, pair_cols)
    d_cat = jnp.concatenate(
        [
            d_values.reshape(rows, inner).astype(jnp.bfloat16),
            d_pairs.astype(jnp.bfloat16),
            d_pre.astype(jnp.bfloat16),
        ],
        axis=1,
    )

    partial_grad = lax.dot_general(
        d_cat, w_all[:, out_cols:], (((1,), (1,)), ((), ())), preferred_element_type=jnp.float32
    )
    grad = scattered_sum(partial_grad, "tp", width).astype(jnp.bfloat16)
    return (output, grad)


def solution(mesh):
    placed = (
        P("ctx", "tp"),
        P("ctx", "tp"),
        P("ctx", "tp"),
        P("ctx", "tp"),
        P("tp"),
        P("tp"),
        P("tp"),
        P("tp", "ctx"),
        P("ctx", "tp"),
    )
    return jax.shard_map(
        per_device,
        mesh=mesh,
        in_specs=placed,
        out_specs=(P("ctx", "tp"), P("ctx", "tp")),
        check_vma=False,
    )
```

```python
import jax
import jax.numpy as jnp
from jax import lax
from jax.sharding import PartitionSpec as P

HEADDIM = 64
STATE = 128
SPAN = 256


HIGH = lax.Precision.HIGHEST


def both_carries(decay, forward, backward, axis):
    devices, position = (lax.axis_size(axis), lax.axis_index(axis))
    heads = decay.shape[0]
    total_a = decay[:, None]
    total_s = forward.reshape(heads, -1)
    total_u = backward.reshape(heads, -1)
    size = total_s.shape[1]
    before_a = jnp.ones_like(total_a)
    before_s = jnp.zeros_like(total_s)
    after_a = jnp.ones_like(total_a)
    after_u = jnp.zeros_like(total_u)
    bit = 1
    while bit < devices:
        message = jnp.concatenate(
            [total_s, total_u, jnp.broadcast_to(total_a, (heads, 128))], axis=1
        )
        got = lax.ppermute(message, axis, [(i, i ^ bit) for i in range(devices)])
        got_s = got[:, :size]
        got_u = got[:, size : 2 * size]
        got_a = got[:, 2 * size : 2 * size + 1]
        lower = (position & bit) != 0
        before_s = jnp.where(lower, before_a * got_s + before_s, before_s)
        before_a = jnp.where(lower, got_a * before_a, before_a)
        after_u = jnp.where(lower, after_u, after_u + after_a * got_u)
        after_a = jnp.where(lower, after_a, after_a * got_a)
        total_s = jnp.where(lower, total_a * got_s + total_s, got_a * total_s + got_s)
        total_u = jnp.where(lower, got_u + got_a * total_u, total_u + total_a * got_u)
        total_a = total_a * got_a
        bit *= 2
    return before_s.reshape(forward.shape), after_u.reshape(backward.shape)


def scattered_sum(partial, axis, width):
    devices, position = (lax.axis_size(axis), lax.axis_index(axis))
    rows = partial.shape[0]
    blocks = partial.reshape(rows, devices, width)
    bit = 1
    while bit < devices:
        count = blocks.shape[1]
        paired = blocks.reshape(rows, count // 2, 2, width)
        mine = (position & bit) != 0
        keep = jnp.where(mine, paired[:, :, 1], paired[:, :, 0])
        send = jnp.where(mine, paired[:, :, 0], paired[:, :, 1])
        blocks = keep + lax.ppermute(send, axis, [(i, i ^ bit) for i in range(devices)])
        bit *= 2
    return blocks.reshape(rows, width)


def ssd_core(values, b_rows, c_rows, step_size, decay_rate, state):
    length, heads, head_dim = values.shape
    groups = b_rows.shape[1]
    per_group = heads // groups
    blocks = length // SPAN
    lower_mask = (jnp.arange(SPAN)[:, None] >= jnp.arange(SPAN)[None, :])[None]

    def blocked(array):
        return array.reshape((blocks, SPAN) + array.shape[1:])

    def ssd_advance(carry, item):
        value_blk, b_blk, c_blk, step_blk = item
        cums = jnp.cumsum(-step_blk * decay_rate[None, :], axis=0)
        diff = cums.T[:, :, None] - cums.T[:, None, :]
        weight = jnp.where(lower_mask, jnp.exp(jnp.where(lower_mask, diff, 0.0)), 0.0)
        scores = jnp.einsum("tgn,sgn->gts", c_blk, b_blk, precision=HIGH)
        scores = jnp.repeat(scores, per_group, axis=0)
        inputs = step_blk[:, :, None] * value_blk
        inside = jnp.einsum("hts,shp->thp", scores * weight, inputs, precision=HIGH)
        c_head = jnp.repeat(c_blk, per_group, axis=1)
        b_head = jnp.repeat(b_blk, per_group, axis=1)
        carried = jnp.exp(cums)[:, :, None] * jnp.einsum(
            "thn,hpn->thp", c_head, carry, precision=HIGH
        )
        tail = jnp.exp(cums[-1][None, :] - cums)
        fresh = jnp.einsum("shp,shn->hpn", tail[:, :, None] * inputs, b_head, precision=HIGH)
        carry = jnp.exp(cums[-1])[:, None, None] * carry + fresh
        return (carry, inside + carried)

    final, outputs = lax.scan(
        jax.checkpoint(ssd_advance),
        state,
        (blocked(values), blocked(b_rows), blocked(c_rows), blocked(step_size)),
    )
    return (outputs.reshape(length, heads, head_dim), final)


def local_states(values, b_rows, step_size, decay_rate):
    length, heads, head_dim = values.shape
    groups = b_rows.shape[1]
    per_group = heads // groups
    blocks = length // SPAN

    def blocked(array):
        return array.reshape((blocks, SPAN) + array.shape[1:])

    def local_advance(carry, item):
        value_blk, b_blk, step_blk = item
        cums = jnp.cumsum(-step_blk * decay_rate[None, :], axis=0)
        tail = jnp.exp(cums[-1][None, :] - cums)
        b_head = jnp.repeat(b_blk, per_group, axis=1)
        inputs = (tail * step_blk)[:, :, None] * value_blk
        fresh = jnp.einsum("shp,shn->hpn", inputs, b_head, precision=HIGH)
        return (jnp.exp(cums[-1])[:, None, None] * carry + fresh, None)

    start = jnp.zeros((heads, head_dim, STATE), jnp.float32)
    final, unused = lax.scan(
        local_advance, start, (blocked(values), blocked(b_rows), blocked(step_size))
    )
    return final


def local_adjoint(d_mixed, c_rows, step_size, decay_rate):
    length, heads, head_dim = d_mixed.shape
    groups = c_rows.shape[1]
    per_group = heads // groups
    blocks = length // SPAN

    def blocked(array):
        return array.reshape((blocks, SPAN) + array.shape[1:])

    def retreat(carry, item):
        grad_blk, c_blk, step_blk = item
        cums = jnp.cumsum(-step_blk * decay_rate[None, :], axis=0)
        c_head = jnp.repeat(c_blk, per_group, axis=1)
        weighted = jnp.exp(cums)[:, :, None] * grad_blk
        term = jnp.einsum("thp,thn->hpn", weighted, c_head, precision=HIGH)
        return (term + jnp.exp(cums[-1])[:, None, None] * carry, None)

    start = jnp.zeros((heads, head_dim, STATE), jnp.float32)
    final, unused = lax.scan(
        retreat, start, (blocked(d_mixed), blocked(c_rows), blocked(step_size)), reverse=True
    )
    return final


def from_each(x, axis):
    devices = lax.axis_size(axis)
    got = [x]
    for k in range(1, devices):
        got.append(lax.ppermute(x, axis, [(i, (i + k) % devices) for i in range(devices)]))
    return got


def doubled_rows(x, axis):
    devices, position = (lax.axis_size(axis), lax.axis_index(axis))
    order = [b for b in range(1, devices.bit_length() - 1)] + [0]
    for b in order:
        bit = 1 << b
        other = lax.ppermute(x, axis, [(i, i ^ bit) for i in range(devices)])
        low = (position & bit) == 0
        x = jnp.where(low, jnp.concatenate([x, other], 0), jnp.concatenate([other, x], 0))
    rows = x.shape[0] // devices
    x = x.reshape((2,) * len(order) + (rows,) + x.shape[1:])
    axes = [len(order) - 1 - order.index(b) for b in reversed(range(len(order)))]
    x = jnp.transpose(x, axes + list(range(len(order), x.ndim)))
    return x.reshape((devices * rows,) + x.shape[len(order) + 1 :])


def row_block(w, index, size):
    return lax.dynamic_slice_in_dim(w, index * size, size, axis=0)


def per_device(tokens, w_in, w_bc, w_dt, dt_bias, decay_rate, skip_gain, w_out, cotangent):
    devices, position = (lax.axis_size("tp"), lax.axis_index("tp"))
    rows, width = tokens.shape
    heads = decay_rate.shape[0]
    inner = w_in.shape[1]
    pair_cols = w_bc.shape[1]
    groups = pair_cols // (2 * STATE)
    out_cols = w_out.shape[0]
    w_proj = lax.all_gather(
        jnp.concatenate([w_in, w_bc, w_dt], axis=1), "ctx", axis=0, tiled=True
    )
    w_back = doubled_rows(w_out.T, "ctx")
    pieces = from_each(jnp.concatenate([tokens, cotangent], axis=1), "tp")
    projected = None
    d_flat = None
    for k in range(devices):
        source = (position - k) % devices
        block = row_block(w_proj, source, width)
        term = jnp.dot(pieces[k][:, :width], block, preferred_element_type=jnp.float32)
        projected = term if projected is None else projected + term
        block = row_block(w_back, source, width)
        term = jnp.dot(pieces[k][:, width:], block, preferred_element_type=jnp.float32)
        d_flat = term if d_flat is None else d_flat + term
    values = projected[:, :inner].astype(jnp.bfloat16)
    pairs = projected[:, inner : inner + pair_cols].astype(jnp.bfloat16)
    pre_step = projected[:, inner + pair_cols :] + dt_bias[None, :]
    step_size = jax.nn.softplus(pre_step)
    value_f = values.astype(jnp.float32).reshape(rows, heads, HEADDIM)
    paired = pairs.astype(jnp.float32).reshape(rows, groups, 2, STATE)
    b_rows = paired[:, :, 0]
    c_rows = paired[:, :, 1]
    end_state = local_states(value_f, b_rows, step_size, decay_rate)
    decay_total = jnp.exp(-jnp.sum(step_size * decay_rate[None, :], axis=0))
    d_mixed = d_flat.reshape(rows, heads, HEADDIM)
    own_adjoint = local_adjoint(d_mixed, c_rows, step_size, decay_rate)
    state_in, adjoint = both_carries(decay_total, end_state, own_adjoint, "ctx")

    def with_state(vals, brows, crows, steps):
        return ssd_core(vals, brows, crows, steps, decay_rate, state_in)

    (core_out, core_end), pullback = jax.vjp(with_state, value_f, b_rows, c_rows, step_size)
    mixed = (
        (core_out + skip_gain[None, :, None] * value_f).reshape(rows, inner).astype(jnp.bfloat16)
    )

    partial_out = lax.dot_general(
        mixed, w_back, (((1,), (1,)), ((), ())), preferred_element_type=jnp.float32
    )
    output = scattered_sum(partial_out, "tp", width).astype(jnp.bfloat16)
    grads = pullback((d_mixed, adjoint))
    d_values = grads[0] + skip_gain[None, :, None] * d_mixed
    d_pre = grads[3] * jax.nn.sigmoid(pre_step)
    d_pairs = jnp.stack([grads[1], grads[2]], axis=2).reshape(rows, pair_cols)
    d_cat = jnp.concatenate(
        [
            d_values.reshape(rows, inner).astype(jnp.bfloat16),
            d_pairs.astype(jnp.bfloat16),
            d_pre.astype(jnp.bfloat16),
        ],
        axis=1,
    )

    partial_grad = lax.dot_general(
        d_cat, w_proj, (((1,), (1,)), ((), ())), preferred_element_type=jnp.float32
    )
    grad = scattered_sum(partial_grad, "tp", width).astype(jnp.bfloat16)
    return (output, grad)


def solution(mesh):
    placed = (
        P("ctx", "tp"),
        P("ctx", "tp"),
        P("ctx", "tp"),
        P("ctx", "tp"),
        P("tp"),
        P("tp"),
        P("tp"),
        P("tp", "ctx"),
        P("ctx", "tp"),
    )
    return jax.shard_map(
        per_device,
        mesh=mesh,
        in_specs=placed,
        out_specs=(P("ctx", "tp"), P("ctx", "tp")),
        check_vma=False,
    )
```

```python
import jax
import jax.numpy as jnp
from jax import lax
from jax.sharding import PartitionSpec as P

HEADDIM = 64
STATE = 128
SPAN = 256


HIGH = lax.Precision.HIGHEST


def both_carries(decay, forward, backward, axis):
    devices, position = (lax.axis_size(axis), lax.axis_index(axis))
    heads = decay.shape[0]
    total_a = decay[:, None]
    total_s = forward.reshape(heads, -1)
    total_u = backward.reshape(heads, -1)
    size = total_s.shape[1]
    before_a = jnp.ones_like(total_a)
    before_s = jnp.zeros_like(total_s)
    after_a = jnp.ones_like(total_a)
    after_u = jnp.zeros_like(total_u)
    bit = 1
    while bit < devices:
        if 2 * bit >= devices:
            lower = (position & bit) != 0
            send = jnp.where(lower, total_u, total_s)
            got = lax.ppermute(send, axis, [(i, i ^ bit) for i in range(devices)])
            before_s = jnp.where(lower, before_a * got + before_s, before_s)
            after_u = jnp.where(lower, after_u, after_u + after_a * got)
            break
        message = jnp.concatenate(
            [total_s, total_u, jnp.broadcast_to(total_a, (heads, 128))], axis=1
        )
        got = lax.ppermute(message, axis, [(i, i ^ bit) for i in range(devices)])
        got_s = got[:, :size]
        got_u = got[:, size : 2 * size]
        got_a = got[:, 2 * size : 2 * size + 1]
        lower = (position & bit) != 0
        before_s = jnp.where(lower, before_a * got_s + before_s, before_s)
        before_a = jnp.where(lower, got_a * before_a, before_a)
        after_u = jnp.where(lower, after_u, after_u + after_a * got_u)
        after_a = jnp.where(lower, after_a, after_a * got_a)
        total_s = jnp.where(lower, total_a * got_s + total_s, got_a * total_s + got_s)
        total_u = jnp.where(lower, got_u + got_a * total_u, total_u + total_a * got_u)
        total_a = total_a * got_a
        bit *= 2
    return before_s.reshape(forward.shape), after_u.reshape(backward.shape)


def scattered_sum(partial, axis, width):
    devices, position = (lax.axis_size(axis), lax.axis_index(axis))
    rows = partial.shape[0]
    blocks = partial.reshape(rows, devices, width)
    bit = 1
    while bit < devices:
        count = blocks.shape[1]
        paired = blocks.reshape(rows, count // 2, 2, width)
        mine = (position & bit) != 0
        keep = jnp.where(mine, paired[:, :, 1], paired[:, :, 0])
        send = jnp.where(mine, paired[:, :, 0], paired[:, :, 1])
        blocks = keep + lax.ppermute(send, axis, [(i, i ^ bit) for i in range(devices)])
        bit *= 2
    return blocks.reshape(rows, width)


def ssd_core(values, b_rows, c_rows, step_size, decay_rate, state):
    length, heads, head_dim = values.shape
    groups = b_rows.shape[1]
    per_group = heads // groups
    blocks = length // SPAN
    lower_mask = (jnp.arange(SPAN)[:, None] >= jnp.arange(SPAN)[None, :])[None]

    def blocked(array):
        return array.reshape((blocks, SPAN) + array.shape[1:])

    def ssd_advance(carry, item):
        value_blk, b_blk, c_blk, step_blk = item
        cums = jnp.cumsum(-step_blk * decay_rate[None, :], axis=0)
        diff = cums.T[:, :, None] - cums.T[:, None, :]
        weight = jnp.where(lower_mask, jnp.exp(jnp.where(lower_mask, diff, 0.0)), 0.0)
        scores = jnp.einsum("tgn,sgn->gts", c_blk, b_blk, precision=HIGH)
        scores = jnp.repeat(scores, per_group, axis=0)
        inputs = step_blk[:, :, None] * value_blk
        inside = jnp.einsum("hts,shp->thp", scores * weight, inputs, precision=HIGH)
        c_head = jnp.repeat(c_blk, per_group, axis=1)
        b_head = jnp.repeat(b_blk, per_group, axis=1)
        carried = jnp.exp(cums)[:, :, None] * jnp.einsum(
            "thn,hpn->thp", c_head, carry, precision=HIGH
        )
        tail = jnp.exp(cums[-1][None, :] - cums)
        fresh = jnp.einsum("shp,shn->hpn", tail[:, :, None] * inputs, b_head, precision=HIGH)
        carry = jnp.exp(cums[-1])[:, None, None] * carry + fresh
        return (carry, inside + carried)

    final, outputs = lax.scan(
        jax.checkpoint(ssd_advance),
        state,
        (blocked(values), blocked(b_rows), blocked(c_rows), blocked(step_size)),
    )
    return (outputs.reshape(length, heads, head_dim), final)


def local_states(values, b_rows, step_size, decay_rate):
    length, heads, head_dim = values.shape
    groups = b_rows.shape[1]
    per_group = heads // groups
    blocks = length // SPAN

    def blocked(array):
        return array.reshape((blocks, SPAN) + array.shape[1:])

    def local_advance(carry, item):
        value_blk, b_blk, step_blk = item
        cums = jnp.cumsum(-step_blk * decay_rate[None, :], axis=0)
        tail = jnp.exp(cums[-1][None, :] - cums)
        b_head = jnp.repeat(b_blk, per_group, axis=1)
        inputs = (tail * step_blk)[:, :, None] * value_blk
        fresh = jnp.einsum("shp,shn->hpn", inputs, b_head, precision=HIGH)
        return (jnp.exp(cums[-1])[:, None, None] * carry + fresh, None)

    start = jnp.zeros((heads, head_dim, STATE), jnp.float32)
    final, unused = lax.scan(
        local_advance, start, (blocked(values), blocked(b_rows), blocked(step_size))
    )
    return final


def local_adjoint(d_mixed, c_rows, step_size, decay_rate):
    length, heads, head_dim = d_mixed.shape
    groups = c_rows.shape[1]
    per_group = heads // groups
    blocks = length // SPAN

    def blocked(array):
        return array.reshape((blocks, SPAN) + array.shape[1:])

    def retreat(carry, item):
        grad_blk, c_blk, step_blk = item
        cums = jnp.cumsum(-step_blk * decay_rate[None, :], axis=0)
        c_head = jnp.repeat(c_blk, per_group, axis=1)
        weighted = jnp.exp(cums)[:, :, None] * grad_blk
        term = jnp.einsum("thp,thn->hpn", weighted, c_head, precision=HIGH)
        return (term + jnp.exp(cums[-1])[:, None, None] * carry, None)

    start = jnp.zeros((heads, head_dim, STATE), jnp.float32)
    final, unused = lax.scan(
        retreat, start, (blocked(d_mixed), blocked(c_rows), blocked(step_size)), reverse=True
    )
    return final


def doubled_rows(x, axis, order):
    devices, position = (lax.axis_size(axis), lax.axis_index(axis))
    for b in order:
        bit = 1 << b
        other = lax.ppermute(x, axis, [(i, i ^ bit) for i in range(devices)])
        low = (position & bit) == 0
        x = jnp.where(low, jnp.concatenate([x, other], 0), jnp.concatenate([other, x], 0))
    rows = x.shape[0] // devices
    x = x.reshape((2,) * len(order) + (rows,) + x.shape[1:])
    axes = [len(order) - 1 - order.index(b) for b in reversed(range(len(order)))]
    x = jnp.transpose(x, axes + list(range(len(order), x.ndim)))
    return x.reshape((devices * rows,) + x.shape[len(order) + 1 :])


def row_block(w, index, size):
    return lax.dynamic_slice_in_dim(w, index * size, size, axis=0)


def per_device(tokens, w_in, w_bc, w_dt, dt_bias, decay_rate, skip_gain, w_out, cotangent):
    devices = lax.axis_size("tp")
    rows, width = tokens.shape
    heads = decay_rate.shape[0]
    inner = w_in.shape[1]
    pair_cols = w_bc.shape[1]
    groups = pair_cols // (2 * STATE)
    out_cols = w_out.shape[0]
    w_all = lax.all_gather(
        jnp.concatenate([w_out.T, w_in, w_bc, w_dt], axis=1), "ctx", axis=0, tiled=True
    )
    bits = devices.bit_length() - 1
    pieces = doubled_rows(
        jnp.concatenate([tokens, cotangent], axis=1), "tp", list(reversed(range(bits)))
    )
    projected = None
    d_flat = None
    for k in range(devices):
        block = w_all[k * width : (k + 1) * width]
        piece = pieces[k * rows : (k + 1) * rows]
        term = jnp.dot(piece[:, :width], block[:, out_cols:], preferred_element_type=jnp.float32)
        projected = term if projected is None else projected + term
        term = jnp.dot(piece[:, width:], block[:, :out_cols], preferred_element_type=jnp.float32)
        d_flat = term if d_flat is None else d_flat + term
    values = projected[:, :inner].astype(jnp.bfloat16)
    pairs = projected[:, inner : inner + pair_cols].astype(jnp.bfloat16)
    pre_step = projected[:, inner + pair_cols :] + dt_bias[None, :]
    step_size = jax.nn.softplus(pre_step)
    value_f = values.astype(jnp.float32).reshape(rows, heads, HEADDIM)
    paired = pairs.astype(jnp.float32).reshape(rows, groups, 2, STATE)
    b_rows = paired[:, :, 0]
    c_rows = paired[:, :, 1]
    end_state = local_states(value_f, b_rows, step_size, decay_rate)
    decay_total = jnp.exp(-jnp.sum(step_size * decay_rate[None, :], axis=0))
    d_mixed = d_flat.reshape(rows, heads, HEADDIM)
    own_adjoint = local_adjoint(d_mixed, c_rows, step_size, decay_rate)
    state_in, adjoint = both_carries(decay_total, end_state, own_adjoint, "ctx")

    def with_state(vals, brows, crows, steps):
        return ssd_core(vals, brows, crows, steps, decay_rate, state_in)

    (core_out, core_end), pullback = jax.vjp(with_state, value_f, b_rows, c_rows, step_size)
    mixed = (
        (core_out + skip_gain[None, :, None] * value_f).reshape(rows, inner).astype(jnp.bfloat16)
    )

    partial_out = lax.dot_general(
        mixed, w_all[:, :out_cols], (((1,), (1,)), ((), ())), preferred_element_type=jnp.float32
    )
    output = scattered_sum(partial_out, "tp", width).astype(jnp.bfloat16)
    grads = pullback((d_mixed, adjoint))
    d_values = grads[0] + skip_gain[None, :, None] * d_mixed
    d_pre = grads[3] * jax.nn.sigmoid(pre_step)
    d_pairs = jnp.stack([grads[1], grads[2]], axis=2).reshape(rows, pair_cols)
    d_cat = jnp.concatenate(
        [
            d_values.reshape(rows, inner).astype(jnp.bfloat16),
            d_pairs.astype(jnp.bfloat16),
            d_pre.astype(jnp.bfloat16),
        ],
        axis=1,
    )

    partial_grad = lax.dot_general(
        d_cat, w_all[:, out_cols:], (((1,), (1,)), ((), ())), preferred_element_type=jnp.float32
    )
    grad = scattered_sum(partial_grad, "tp", width).astype(jnp.bfloat16)
    return (output, grad)


def solution(mesh):
    placed = (
        P("ctx", "tp"),
        P("ctx", "tp"),
        P("ctx", "tp"),
        P("ctx", "tp"),
        P("tp"),
        P("tp"),
        P("tp"),
        P("tp", "ctx"),
        P("ctx", "tp"),
    )
    return jax.shard_map(
        per_device,
        mesh=mesh,
        in_specs=placed,
        out_specs=(P("ctx", "tp"), P("ctx", "tp")),
        check_vma=False,
    )
```

```python
import jax
import jax.numpy as jnp
from jax import lax
from jax.sharding import Mesh, PartitionSpec as P

HEADDIM = 64
STATE = 128
SPAN = 256


HIGH = lax.Precision.HIGHEST
CTX = ("rest", "core")


def both_carries(decay, forward, backward, axis):
    devices, position = (lax.axis_size(axis), lax.axis_index(axis))
    heads = decay.shape[0]
    total_a = decay[:, None]
    total_s = forward.reshape(heads, -1)
    total_u = backward.reshape(heads, -1)
    size = total_s.shape[1]
    before_a = jnp.ones_like(total_a)
    before_s = jnp.zeros_like(total_s)
    after_a = jnp.ones_like(total_a)
    after_u = jnp.zeros_like(total_u)
    bit = 1
    while bit < devices:
        if 2 * bit >= devices:
            lower = (position & bit) != 0
            send = jnp.where(lower, total_u, total_s)
            got = lax.ppermute(send, axis, [(i, i ^ bit) for i in range(devices)])
            before_s = jnp.where(lower, before_a * got + before_s, before_s)
            after_u = jnp.where(lower, after_u, after_u + after_a * got)
            break
        message = jnp.concatenate(
            [total_s, total_u, jnp.broadcast_to(total_a, (heads, 128))], axis=1
        )
        got = lax.ppermute(message, axis, [(i, i ^ bit) for i in range(devices)])
        got_s = got[:, :size]
        got_u = got[:, size : 2 * size]
        got_a = got[:, 2 * size : 2 * size + 1]
        lower = (position & bit) != 0
        before_s = jnp.where(lower, before_a * got_s + before_s, before_s)
        before_a = jnp.where(lower, got_a * before_a, before_a)
        after_u = jnp.where(lower, after_u, after_u + after_a * got_u)
        after_a = jnp.where(lower, after_a, after_a * got_a)
        total_s = jnp.where(lower, total_a * got_s + total_s, got_a * total_s + got_s)
        total_u = jnp.where(lower, got_u + got_a * total_u, total_u + total_a * got_u)
        total_a = total_a * got_a
        bit *= 2
    return before_s.reshape(forward.shape), after_u.reshape(backward.shape)


def scattered_sum(partial, axis, width):
    devices, position = (lax.axis_size(axis), lax.axis_index(axis))
    rows = partial.shape[0]
    blocks = partial.reshape(rows, devices, width)
    bit = 1
    while bit < devices:
        count = blocks.shape[1]
        paired = blocks.reshape(rows, count // 2, 2, width)
        mine = (position & bit) != 0
        keep = jnp.where(mine, paired[:, :, 1], paired[:, :, 0])
        send = jnp.where(mine, paired[:, :, 0], paired[:, :, 1])
        blocks = keep + lax.ppermute(send, axis, [(i, i ^ bit) for i in range(devices)])
        bit *= 2
    return blocks.reshape(rows, width)


def ssd_core(values, b_rows, c_rows, step_size, decay_rate, state):
    length, heads, head_dim = values.shape
    groups = b_rows.shape[1]
    per_group = heads // groups
    blocks = length // SPAN
    lower_mask = (jnp.arange(SPAN)[:, None] >= jnp.arange(SPAN)[None, :])[None]

    def blocked(array):
        return array.reshape((blocks, SPAN) + array.shape[1:])

    def ssd_advance(carry, item):
        value_blk, b_blk, c_blk, step_blk = item
        cums = jnp.cumsum(-step_blk * decay_rate[None, :], axis=0)
        diff = cums.T[:, :, None] - cums.T[:, None, :]
        weight = jnp.where(lower_mask, jnp.exp(jnp.where(lower_mask, diff, 0.0)), 0.0)
        scores = jnp.einsum("tgn,sgn->gts", c_blk, b_blk, precision=HIGH)
        scores = jnp.repeat(scores, per_group, axis=0)
        inputs = step_blk[:, :, None] * value_blk
        inside = jnp.einsum("hts,shp->thp", scores * weight, inputs, precision=HIGH)
        c_head = jnp.repeat(c_blk, per_group, axis=1)
        b_head = jnp.repeat(b_blk, per_group, axis=1)
        carried = jnp.exp(cums)[:, :, None] * jnp.einsum(
            "thn,hpn->thp", c_head, carry, precision=HIGH
        )
        tail = jnp.exp(cums[-1][None, :] - cums)
        fresh = jnp.einsum("shp,shn->hpn", tail[:, :, None] * inputs, b_head, precision=HIGH)
        carry = jnp.exp(cums[-1])[:, None, None] * carry + fresh
        return (carry, inside + carried)

    final, outputs = lax.scan(
        jax.checkpoint(ssd_advance),
        state,
        (blocked(values), blocked(b_rows), blocked(c_rows), blocked(step_size)),
    )
    return (outputs.reshape(length, heads, head_dim), final)


def local_states(values, b_rows, step_size, decay_rate):
    length, heads, head_dim = values.shape
    groups = b_rows.shape[1]
    per_group = heads // groups
    blocks = length // SPAN

    def blocked(array):
        return array.reshape((blocks, SPAN) + array.shape[1:])

    def local_advance(carry, item):
        value_blk, b_blk, step_blk = item
        cums = jnp.cumsum(-step_blk * decay_rate[None, :], axis=0)
        tail = jnp.exp(cums[-1][None, :] - cums)
        b_head = jnp.repeat(b_blk, per_group, axis=1)
        inputs = (tail * step_blk)[:, :, None] * value_blk
        fresh = jnp.einsum("shp,shn->hpn", inputs, b_head, precision=HIGH)
        return (jnp.exp(cums[-1])[:, None, None] * carry + fresh, None)

    start = jnp.zeros((heads, head_dim, STATE), jnp.float32)
    final, unused = lax.scan(
        local_advance, start, (blocked(values), blocked(b_rows), blocked(step_size))
    )
    return final


def local_adjoint(d_mixed, c_rows, step_size, decay_rate):
    length, heads, head_dim = d_mixed.shape
    groups = c_rows.shape[1]
    per_group = heads // groups
    blocks = length // SPAN

    def blocked(array):
        return array.reshape((blocks, SPAN) + array.shape[1:])

    def retreat(carry, item):
        grad_blk, c_blk, step_blk = item
        cums = jnp.cumsum(-step_blk * decay_rate[None, :], axis=0)
        c_head = jnp.repeat(c_blk, per_group, axis=1)
        weighted = jnp.exp(cums)[:, :, None] * grad_blk
        term = jnp.einsum("thp,thn->hpn", weighted, c_head, precision=HIGH)
        return (term + jnp.exp(cums[-1])[:, None, None] * carry, None)

    start = jnp.zeros((heads, head_dim, STATE), jnp.float32)
    final, unused = lax.scan(
        retreat, start, (blocked(d_mixed), blocked(c_rows), blocked(step_size)), reverse=True
    )
    return final


def doubled_rows(x, axis, order):
    devices, position = (lax.axis_size(axis), lax.axis_index(axis))
    for b in order:
        bit = 1 << b
        other = lax.ppermute(x, axis, [(i, i ^ bit) for i in range(devices)])
        low = (position & bit) == 0
        x = jnp.where(low, jnp.concatenate([x, other], 0), jnp.concatenate([other, x], 0))
    rows = x.shape[0] // devices
    x = x.reshape((2,) * len(order) + (rows,) + x.shape[1:])
    axes = [len(order) - 1 - order.index(b) for b in reversed(range(len(order)))]
    x = jnp.transpose(x, axes + list(range(len(order), x.ndim)))
    return x.reshape((devices * rows,) + x.shape[len(order) + 1 :])


def row_block(w, index, size):
    return lax.dynamic_slice_in_dim(w, index * size, size, axis=0)


def per_device(tokens, w_in, w_bc, w_dt, dt_bias, decay_rate, skip_gain, w_out, cotangent):
    devices = lax.axis_size("tp")
    rows, width = tokens.shape
    heads = decay_rate.shape[0]
    inner = w_in.shape[1]
    pair_cols = w_bc.shape[1]
    groups = pair_cols // (2 * STATE)
    out_cols = w_out.shape[0]
    w_own = jnp.concatenate([w_out.T, w_in, w_bc, w_dt], axis=1)
    w_same = lax.all_gather(w_own, "rest", axis=0, tiled=True)
    w_other = lax.ppermute(w_same, "core", [(0, 1), (1, 0)])
    core = lax.axis_index("core")
    pair = (w_same.shape[0] // w_own.shape[0], 1, w_own.shape[0], w_own.shape[1])
    low, high = (w_same.reshape(pair), w_other.reshape(pair))
    w_all = jnp.where(
        core == 0, jnp.concatenate([low, high], axis=1), jnp.concatenate([high, low], axis=1)
    ).reshape(-1, w_own.shape[1])
    bits = devices.bit_length() - 1
    pieces = doubled_rows(
        jnp.concatenate([tokens, cotangent], axis=1), "tp", list(reversed(range(bits)))
    )
    projected = None
    d_flat = None
    for k in range(devices):
        block = w_all[k * width : (k + 1) * width]
        piece = pieces[k * rows : (k + 1) * rows]
        term = jnp.dot(piece[:, :width], block[:, out_cols:], preferred_element_type=jnp.float32)
        projected = term if projected is None else projected + term
        term = jnp.dot(piece[:, width:], block[:, :out_cols], preferred_element_type=jnp.float32)
        d_flat = term if d_flat is None else d_flat + term
    values = projected[:, :inner].astype(jnp.bfloat16)
    pairs = projected[:, inner : inner + pair_cols].astype(jnp.bfloat16)
    pre_step = projected[:, inner + pair_cols :] + dt_bias[None, :]
    step_size = jax.nn.softplus(pre_step)
    value_f = values.astype(jnp.float32).reshape(rows, heads, HEADDIM)
    paired = pairs.astype(jnp.float32).reshape(rows, groups, 2, STATE)
    b_rows = paired[:, :, 0]
    c_rows = paired[:, :, 1]
    end_state = local_states(value_f, b_rows, step_size, decay_rate)
    decay_total = jnp.exp(-jnp.sum(step_size * decay_rate[None, :], axis=0))
    d_mixed = d_flat.reshape(rows, heads, HEADDIM)
    own_adjoint = local_adjoint(d_mixed, c_rows, step_size, decay_rate)
    state_in, adjoint = both_carries(decay_total, end_state, own_adjoint, CTX)

    def with_state(vals, brows, crows, steps):
        return ssd_core(vals, brows, crows, steps, decay_rate, state_in)

    (core_out, core_end), pullback = jax.vjp(with_state, value_f, b_rows, c_rows, step_size)
    mixed = (
        (core_out + skip_gain[None, :, None] * value_f).reshape(rows, inner).astype(jnp.bfloat16)
    )

    partial_out = lax.dot_general(
        mixed, w_all[:, :out_cols], (((1,), (1,)), ((), ())), preferred_element_type=jnp.float32
    )
    output = scattered_sum(partial_out, "tp", width).astype(jnp.bfloat16)
    grads = pullback((d_mixed, adjoint))
    d_values = grads[0] + skip_gain[None, :, None] * d_mixed
    d_pre = grads[3] * jax.nn.sigmoid(pre_step)
    d_pairs = jnp.stack([grads[1], grads[2]], axis=2).reshape(rows, pair_cols)
    d_cat = jnp.concatenate(
        [
            d_values.reshape(rows, inner).astype(jnp.bfloat16),
            d_pairs.astype(jnp.bfloat16),
            d_pre.astype(jnp.bfloat16),
        ],
        axis=1,
    )

    partial_grad = lax.dot_general(
        d_cat, w_all[:, out_cols:], (((1,), (1,)), ((), ())), preferred_element_type=jnp.float32
    )
    grad = scattered_sum(partial_grad, "tp", width).astype(jnp.bfloat16)
    return (output, grad)


def solution(mesh):
    ctx, tp = (mesh.shape["ctx"], mesh.shape["tp"])
    split = Mesh(mesh.devices.reshape(ctx // 2, 2, tp), ("rest", "core", "tp"))
    rows = P(CTX, "tp")
    placed = (rows, rows, rows, rows, P("tp"), P("tp"), P("tp"), P("tp", CTX), rows)
    return jax.shard_map(
        per_device,
        mesh=split,
        in_specs=placed,
        out_specs=(rows, rows),
        check_vma=False,
    )
```

```python
import jax
import jax.numpy as jnp
from jax import lax
from jax.sharding import PartitionSpec as P

HEADDIM = 64
STATE = 128
SPAN = 256


HIGH = lax.Precision.HIGHEST
RING = 4


def both_carries(decay, forward, backward, axis):
    devices, position = (lax.axis_size(axis), lax.axis_index(axis))
    heads = decay.shape[0]
    total_a = decay[:, None]
    total_s = forward.reshape(heads, -1)
    total_u = backward.reshape(heads, -1)
    size = total_s.shape[1]
    before_a = jnp.ones_like(total_a)
    before_s = jnp.zeros_like(total_s)
    after_a = jnp.ones_like(total_a)
    after_u = jnp.zeros_like(total_u)
    bit = 1
    while bit < devices:
        if 2 * bit >= devices:
            lower = (position & bit) != 0
            send = jnp.where(lower, total_u, total_s)
            got = lax.ppermute(send, axis, [(i, i ^ bit) for i in range(devices)])
            before_s = jnp.where(lower, before_a * got + before_s, before_s)
            after_u = jnp.where(lower, after_u, after_u + after_a * got)
            break
        message = jnp.concatenate(
            [total_s, total_u, jnp.broadcast_to(total_a, (heads, 128))], axis=1
        )
        got = lax.ppermute(message, axis, [(i, i ^ bit) for i in range(devices)])
        got_s = got[:, :size]
        got_u = got[:, size : 2 * size]
        got_a = got[:, 2 * size : 2 * size + 1]
        lower = (position & bit) != 0
        before_s = jnp.where(lower, before_a * got_s + before_s, before_s)
        before_a = jnp.where(lower, got_a * before_a, before_a)
        after_u = jnp.where(lower, after_u, after_u + after_a * got_u)
        after_a = jnp.where(lower, after_a, after_a * got_a)
        total_s = jnp.where(lower, total_a * got_s + total_s, got_a * total_s + got_s)
        total_u = jnp.where(lower, got_u + got_a * total_u, total_u + total_a * got_u)
        total_a = total_a * got_a
        bit *= 2
    return before_s.reshape(forward.shape), after_u.reshape(backward.shape)


def scattered_sum(partial, rows_axis, axis, width):
    chains, devices = (lax.axis_size(rows_axis), lax.axis_size(axis))
    chain, position = (lax.axis_index(rows_axis), lax.axis_index(axis))
    ring = RING if devices % RING == 0 else 1

    def label(t, turn):
        return t - t % ring + (t + turn) % ring

    def place(lab, turn):
        return lab - lab % ring + (lab - turn) % ring

    turn = chain % 2
    mine_label = label(position, turn)
    order = [place(lab, 1) for lab in range(devices)]
    rows = partial.shape[0]
    blocks = partial.reshape(rows, devices, width)
    blocks = jnp.where(turn == 1, blocks[:, order], blocks)
    bit = 1
    while bit < devices:
        count = blocks.shape[1]
        paired = blocks.reshape(rows, count // 2, 2, width)
        mine = (mine_label & bit) != 0
        keep = jnp.where(mine, paired[:, :, 1], paired[:, :, 0])
        send = jnp.where(mine, paired[:, :, 0], paired[:, :, 1])
        pairs = []
        for c in range(chains):
            for t in range(devices):
                partner = place(label(t, c % 2) ^ bit, c % 2)
                pairs.append((c * devices + t, c * devices + partner))
        blocks = keep + lax.ppermute(send, (rows_axis, axis), pairs)
        bit *= 2
    return blocks.reshape(rows, width)


def ssd_core(values, b_rows, c_rows, step_size, decay_rate, state):
    length, heads, head_dim = values.shape
    groups = b_rows.shape[1]
    per_group = heads // groups
    blocks = length // SPAN
    lower_mask = (jnp.arange(SPAN)[:, None] >= jnp.arange(SPAN)[None, :])[None]

    def blocked(array):
        return array.reshape((blocks, SPAN) + array.shape[1:])

    def ssd_advance(carry, item):
        value_blk, b_blk, c_blk, step_blk = item
        cums = jnp.cumsum(-step_blk * decay_rate[None, :], axis=0)
        diff = cums.T[:, :, None] - cums.T[:, None, :]
        weight = jnp.where(lower_mask, jnp.exp(jnp.where(lower_mask, diff, 0.0)), 0.0)
        scores = jnp.einsum("tgn,sgn->gts", c_blk, b_blk, precision=HIGH)
        scores = jnp.repeat(scores, per_group, axis=0)
        inputs = step_blk[:, :, None] * value_blk
        inside = jnp.einsum("hts,shp->thp", scores * weight, inputs, precision=HIGH)
        c_head = jnp.repeat(c_blk, per_group, axis=1)
        b_head = jnp.repeat(b_blk, per_group, axis=1)
        carried = jnp.exp(cums)[:, :, None] * jnp.einsum(
            "thn,hpn->thp", c_head, carry, precision=HIGH
        )
        tail = jnp.exp(cums[-1][None, :] - cums)
        fresh = jnp.einsum("shp,shn->hpn", tail[:, :, None] * inputs, b_head, precision=HIGH)
        carry = jnp.exp(cums[-1])[:, None, None] * carry + fresh
        return (carry, inside + carried)

    final, outputs = lax.scan(
        jax.checkpoint(ssd_advance),
        state,
        (blocked(values), blocked(b_rows), blocked(c_rows), blocked(step_size)),
    )
    return (outputs.reshape(length, heads, head_dim), final)


def local_states(values, b_rows, step_size, decay_rate):
    length, heads, head_dim = values.shape
    groups = b_rows.shape[1]
    per_group = heads // groups
    blocks = length // SPAN

    def blocked(array):
        return array.reshape((blocks, SPAN) + array.shape[1:])

    def local_advance(carry, item):
        value_blk, b_blk, step_blk = item
        cums = jnp.cumsum(-step_blk * decay_rate[None, :], axis=0)
        tail = jnp.exp(cums[-1][None, :] - cums)
        b_head = jnp.repeat(b_blk, per_group, axis=1)
        inputs = (tail * step_blk)[:, :, None] * value_blk
        fresh = jnp.einsum("shp,shn->hpn", inputs, b_head, precision=HIGH)
        return (jnp.exp(cums[-1])[:, None, None] * carry + fresh, None)

    start = jnp.zeros((heads, head_dim, STATE), jnp.float32)
    final, unused = lax.scan(
        local_advance, start, (blocked(values), blocked(b_rows), blocked(step_size))
    )
    return final


def local_adjoint(d_mixed, c_rows, step_size, decay_rate):
    length, heads, head_dim = d_mixed.shape
    groups = c_rows.shape[1]
    per_group = heads // groups
    blocks = length // SPAN

    def blocked(array):
        return array.reshape((blocks, SPAN) + array.shape[1:])

    def retreat(carry, item):
        grad_blk, c_blk, step_blk = item
        cums = jnp.cumsum(-step_blk * decay_rate[None, :], axis=0)
        c_head = jnp.repeat(c_blk, per_group, axis=1)
        weighted = jnp.exp(cums)[:, :, None] * grad_blk
        term = jnp.einsum("thp,thn->hpn", weighted, c_head, precision=HIGH)
        return (term + jnp.exp(cums[-1])[:, None, None] * carry, None)

    start = jnp.zeros((heads, head_dim, STATE), jnp.float32)
    final, unused = lax.scan(
        retreat, start, (blocked(d_mixed), blocked(c_rows), blocked(step_size)), reverse=True
    )
    return final


def doubled_rows(x, axis, order):
    devices, position = (lax.axis_size(axis), lax.axis_index(axis))
    for b in order:
        bit = 1 << b
        other = lax.ppermute(x, axis, [(i, i ^ bit) for i in range(devices)])
        low = (position & bit) == 0
        x = jnp.where(low, jnp.concatenate([x, other], 0), jnp.concatenate([other, x], 0))
    rows = x.shape[0] // devices
    x = x.reshape((2,) * len(order) + (rows,) + x.shape[1:])
    axes = [len(order) - 1 - order.index(b) for b in reversed(range(len(order)))]
    x = jnp.transpose(x, axes + list(range(len(order), x.ndim)))
    return x.reshape((devices * rows,) + x.shape[len(order) + 1 :])


def row_block(w, index, size):
    return lax.dynamic_slice_in_dim(w, index * size, size, axis=0)


def per_device(tokens, w_in, w_bc, w_dt, dt_bias, decay_rate, skip_gain, w_out, cotangent):
    devices = lax.axis_size("tp")
    rows, width = tokens.shape
    heads = decay_rate.shape[0]
    inner = w_in.shape[1]
    pair_cols = w_bc.shape[1]
    groups = pair_cols // (2 * STATE)
    out_cols = w_out.shape[0]
    w_all = lax.all_gather(
        jnp.concatenate([w_out.T, w_in, w_bc, w_dt], axis=1), "ctx", axis=0, tiled=True
    )
    bits = devices.bit_length() - 1
    pieces = doubled_rows(
        jnp.concatenate([tokens, cotangent], axis=1), "tp", list(reversed(range(bits)))
    )
    projected = None
    d_flat = None
    for k in range(devices):
        block = w_all[k * width : (k + 1) * width]
        piece = pieces[k * rows : (k + 1) * rows]
        term = jnp.dot(piece[:, :width], block[:, out_cols:], preferred_element_type=jnp.float32)
        projected = term if projected is None else projected + term
        term = jnp.dot(piece[:, width:], block[:, :out_cols], preferred_element_type=jnp.float32)
        d_flat = term if d_flat is None else d_flat + term
    values = projected[:, :inner].astype(jnp.bfloat16)
    pairs = projected[:, inner : inner + pair_cols].astype(jnp.bfloat16)
    pre_step = projected[:, inner + pair_cols :] + dt_bias[None, :]
    step_size = jax.nn.softplus(pre_step)
    value_f = values.astype(jnp.float32).reshape(rows, heads, HEADDIM)
    paired = pairs.astype(jnp.float32).reshape(rows, groups, 2, STATE)
    b_rows = paired[:, :, 0]
    c_rows = paired[:, :, 1]
    end_state = local_states(value_f, b_rows, step_size, decay_rate)
    decay_total = jnp.exp(-jnp.sum(step_size * decay_rate[None, :], axis=0))
    d_mixed = d_flat.reshape(rows, heads, HEADDIM)
    own_adjoint = local_adjoint(d_mixed, c_rows, step_size, decay_rate)
    state_in, adjoint = both_carries(decay_total, end_state, own_adjoint, "ctx")

    def with_state(vals, brows, crows, steps):
        return ssd_core(vals, brows, crows, steps, decay_rate, state_in)

    (core_out, core_end), pullback = jax.vjp(with_state, value_f, b_rows, c_rows, step_size)
    mixed = (
        (core_out + skip_gain[None, :, None] * value_f).reshape(rows, inner).astype(jnp.bfloat16)
    )

    partial_out = lax.dot_general(
        mixed, w_all[:, :out_cols], (((1,), (1,)), ((), ())), preferred_element_type=jnp.float32
    )
    output = scattered_sum(partial_out, "ctx", "tp", width).astype(jnp.bfloat16)
    grads = pullback((d_mixed, adjoint))
    d_values = grads[0] + skip_gain[None, :, None] * d_mixed
    d_pre = grads[3] * jax.nn.sigmoid(pre_step)
    d_pairs = jnp.stack([grads[1], grads[2]], axis=2).reshape(rows, pair_cols)
    d_cat = jnp.concatenate(
        [
            d_values.reshape(rows, inner).astype(jnp.bfloat16),
            d_pairs.astype(jnp.bfloat16),
            d_pre.astype(jnp.bfloat16),
        ],
        axis=1,
    )

    partial_grad = lax.dot_general(
        d_cat, w_all[:, out_cols:], (((1,), (1,)), ((), ())), preferred_element_type=jnp.float32
    )
    grad = scattered_sum(partial_grad, "ctx", "tp", width).astype(jnp.bfloat16)
    return (output, grad)


def solution(mesh):
    placed = (
        P("ctx", "tp"),
        P("ctx", "tp"),
        P("ctx", "tp"),
        P("ctx", "tp"),
        P("tp"),
        P("tp"),
        P("tp"),
        P("tp", "ctx"),
        P("ctx", "tp"),
    )
    return jax.shard_map(
        per_device,
        mesh=mesh,
        in_specs=placed,
        out_specs=(P("ctx", "tp"), P("ctx", "tp")),
        check_vma=False,
    )
```

```python
import jax
import jax.numpy as jnp
from jax import lax
from jax.sharding import PartitionSpec as P

HEADDIM = 64
STATE = 128
SPAN = 256


HIGH = lax.Precision.HIGHEST
RING = 4


def both_carries(decay, forward, backward, axis):
    devices, position = (lax.axis_size(axis), lax.axis_index(axis))
    heads = decay.shape[0]
    total_a = decay[:, None]
    total_s = forward.reshape(heads, -1)
    total_u = backward.reshape(heads, -1)
    size = total_s.shape[1]
    before_a = jnp.ones_like(total_a)
    before_s = jnp.zeros_like(total_s)
    after_a = jnp.ones_like(total_a)
    after_u = jnp.zeros_like(total_u)
    bit = 1
    while bit < devices:
        if 2 * bit >= devices:
            lower = (position & bit) != 0
            send = jnp.where(lower, total_u, total_s)
            got = lax.ppermute(send, axis, [(i, i ^ bit) for i in range(devices)])
            before_s = jnp.where(lower, before_a * got + before_s, before_s)
            after_u = jnp.where(lower, after_u, after_u + after_a * got)
            break
        message = jnp.concatenate(
            [total_s, total_u, jnp.broadcast_to(total_a, (heads, 128))], axis=1
        )
        got = lax.ppermute(message, axis, [(i, i ^ bit) for i in range(devices)])
        got_s = got[:, :size]
        got_u = got[:, size : 2 * size]
        got_a = got[:, 2 * size : 2 * size + 1]
        lower = (position & bit) != 0
        before_s = jnp.where(lower, before_a * got_s + before_s, before_s)
        before_a = jnp.where(lower, got_a * before_a, before_a)
        after_u = jnp.where(lower, after_u, after_u + after_a * got_u)
        after_a = jnp.where(lower, after_a, after_a * got_a)
        total_s = jnp.where(lower, total_a * got_s + total_s, got_a * total_s + got_s)
        total_u = jnp.where(lower, got_u + got_a * total_u, total_u + total_a * got_u)
        total_a = total_a * got_a
        bit *= 2
    return before_s.reshape(forward.shape), after_u.reshape(backward.shape)


def scattered_sum(part_of, rows_axis, axis, width):
    chains, devices = (lax.axis_size(rows_axis), lax.axis_size(axis))
    chain, position = (lax.axis_index(rows_axis), lax.axis_index(axis))
    ring = RING if devices % RING == 0 else 1

    def label(t, turn):
        return t - t % ring + (t + turn) % ring

    def place(lab, turn):
        return lab - lab % ring + (lab - turn) % ring

    turn = chain % 2
    mine_label = label(position, turn)
    blocks = jnp.stack([part_of(place(lab, turn)) for lab in range(devices)], axis=1)
    rows = blocks.shape[0]
    bit = 1
    while bit < devices:
        count = blocks.shape[1]
        paired = blocks.reshape(rows, count // 2, 2, width)
        mine = (mine_label & bit) != 0
        keep = jnp.where(mine, paired[:, :, 1], paired[:, :, 0])
        send = jnp.where(mine, paired[:, :, 0], paired[:, :, 1])
        pairs = []
        for c in range(chains):
            for t in range(devices):
                partner = place(label(t, c % 2) ^ bit, c % 2)
                pairs.append((c * devices + t, c * devices + partner))
        blocks = keep + lax.ppermute(send, (rows_axis, axis), pairs)
        bit *= 2
    return blocks.reshape(rows, width)


def ssd_core(values, b_rows, c_rows, step_size, decay_rate, state):
    length, heads, head_dim = values.shape
    groups = b_rows.shape[1]
    per_group = heads // groups
    blocks = length // SPAN
    lower_mask = (jnp.arange(SPAN)[:, None] >= jnp.arange(SPAN)[None, :])[None]

    def blocked(array):
        return array.reshape((blocks, SPAN) + array.shape[1:])

    def ssd_advance(carry, item):
        value_blk, b_blk, c_blk, step_blk = item
        cums = jnp.cumsum(-step_blk * decay_rate[None, :], axis=0)
        diff = cums.T[:, :, None] - cums.T[:, None, :]
        weight = jnp.where(lower_mask, jnp.exp(jnp.where(lower_mask, diff, 0.0)), 0.0)
        scores = jnp.einsum("tgn,sgn->gts", c_blk, b_blk, precision=HIGH)
        scores = jnp.repeat(scores, per_group, axis=0)
        inputs = step_blk[:, :, None] * value_blk
        inside = jnp.einsum("hts,shp->thp", scores * weight, inputs, precision=HIGH)
        c_head = jnp.repeat(c_blk, per_group, axis=1)
        b_head = jnp.repeat(b_blk, per_group, axis=1)
        carried = jnp.exp(cums)[:, :, None] * jnp.einsum(
            "thn,hpn->thp", c_head, carry, precision=HIGH
        )
        tail = jnp.exp(cums[-1][None, :] - cums)
        fresh = jnp.einsum("shp,shn->hpn", tail[:, :, None] * inputs, b_head, precision=HIGH)
        carry = jnp.exp(cums[-1])[:, None, None] * carry + fresh
        return (carry, inside + carried)

    final, outputs = lax.scan(
        jax.checkpoint(ssd_advance),
        state,
        (blocked(values), blocked(b_rows), blocked(c_rows), blocked(step_size)),
    )
    return (outputs.reshape(length, heads, head_dim), final)


def local_states(values, b_rows, step_size, decay_rate):
    length, heads, head_dim = values.shape
    groups = b_rows.shape[1]
    per_group = heads // groups
    blocks = length // SPAN

    def blocked(array):
        return array.reshape((blocks, SPAN) + array.shape[1:])

    def local_advance(carry, item):
        value_blk, b_blk, step_blk = item
        cums = jnp.cumsum(-step_blk * decay_rate[None, :], axis=0)
        tail = jnp.exp(cums[-1][None, :] - cums)
        b_head = jnp.repeat(b_blk, per_group, axis=1)
        inputs = (tail * step_blk)[:, :, None] * value_blk
        fresh = jnp.einsum("shp,shn->hpn", inputs, b_head, precision=HIGH)
        return (jnp.exp(cums[-1])[:, None, None] * carry + fresh, None)

    start = jnp.zeros((heads, head_dim, STATE), jnp.float32)
    final, unused = lax.scan(
        local_advance, start, (blocked(values), blocked(b_rows), blocked(step_size))
    )
    return final


def local_adjoint(d_mixed, c_rows, step_size, decay_rate):
    length, heads, head_dim = d_mixed.shape
    groups = c_rows.shape[1]
    per_group = heads // groups
    blocks = length // SPAN

    def blocked(array):
        return array.reshape((blocks, SPAN) + array.shape[1:])

    def retreat(carry, item):
        grad_blk, c_blk, step_blk = item
        cums = jnp.cumsum(-step_blk * decay_rate[None, :], axis=0)
        c_head = jnp.repeat(c_blk, per_group, axis=1)
        weighted = jnp.exp(cums)[:, :, None] * grad_blk
        term = jnp.einsum("thp,thn->hpn", weighted, c_head, precision=HIGH)
        return (term + jnp.exp(cums[-1])[:, None, None] * carry, None)

    start = jnp.zeros((heads, head_dim, STATE), jnp.float32)
    final, unused = lax.scan(
        retreat, start, (blocked(d_mixed), blocked(c_rows), blocked(step_size)), reverse=True
    )
    return final


def doubled_rows(x, axis, order):
    devices, position = (lax.axis_size(axis), lax.axis_index(axis))
    for b in order:
        bit = 1 << b
        other = lax.ppermute(x, axis, [(i, i ^ bit) for i in range(devices)])
        low = (position & bit) == 0
        x = jnp.where(low, jnp.concatenate([x, other], 0), jnp.concatenate([other, x], 0))
    rows = x.shape[0] // devices
    x = x.reshape((2,) * len(order) + (rows,) + x.shape[1:])
    axes = [len(order) - 1 - order.index(b) for b in reversed(range(len(order)))]
    x = jnp.transpose(x, axes + list(range(len(order), x.ndim)))
    return x.reshape((devices * rows,) + x.shape[len(order) + 1 :])


def row_block(w, index, size):
    return lax.dynamic_slice_in_dim(w, index * size, size, axis=0)


def per_device(tokens, w_in, w_bc, w_dt, dt_bias, decay_rate, skip_gain, w_out, cotangent):
    devices = lax.axis_size("tp")
    rows, width = tokens.shape
    heads = decay_rate.shape[0]
    inner = w_in.shape[1]
    pair_cols = w_bc.shape[1]
    groups = pair_cols // (2 * STATE)
    out_cols = w_out.shape[0]
    w_all = lax.all_gather(
        jnp.concatenate([w_out.T, w_in, w_bc, w_dt], axis=1), "ctx", axis=0, tiled=True
    )
    bits = devices.bit_length() - 1
    pieces = doubled_rows(
        jnp.concatenate([tokens, cotangent], axis=1), "tp", list(reversed(range(bits)))
    )
    projected = None
    d_flat = None
    for k in range(devices):
        block = w_all[k * width : (k + 1) * width]
        piece = pieces[k * rows : (k + 1) * rows]
        term = jnp.dot(piece[:, :width], block[:, out_cols:], preferred_element_type=jnp.float32)
        projected = term if projected is None else projected + term
        term = jnp.dot(piece[:, width:], block[:, :out_cols], preferred_element_type=jnp.float32)
        d_flat = term if d_flat is None else d_flat + term
    values = projected[:, :inner].astype(jnp.bfloat16)
    pairs = projected[:, inner : inner + pair_cols].astype(jnp.bfloat16)
    pre_step = projected[:, inner + pair_cols :] + dt_bias[None, :]
    step_size = jax.nn.softplus(pre_step)
    value_f = values.astype(jnp.float32).reshape(rows, heads, HEADDIM)
    paired = pairs.astype(jnp.float32).reshape(rows, groups, 2, STATE)
    b_rows = paired[:, :, 0]
    c_rows = paired[:, :, 1]
    end_state = local_states(value_f, b_rows, step_size, decay_rate)
    decay_total = jnp.exp(-jnp.sum(step_size * decay_rate[None, :], axis=0))
    d_mixed = d_flat.reshape(rows, heads, HEADDIM)
    own_adjoint = local_adjoint(d_mixed, c_rows, step_size, decay_rate)
    state_in, adjoint = both_carries(decay_total, end_state, own_adjoint, "ctx")

    def with_state(vals, brows, crows, steps):
        return ssd_core(vals, brows, crows, steps, decay_rate, state_in)

    (core_out, core_end), pullback = jax.vjp(with_state, value_f, b_rows, c_rows, step_size)
    mixed = (
        (core_out + skip_gain[None, :, None] * value_f).reshape(rows, inner).astype(jnp.bfloat16)
    )

    def out_part(dest):
        block = row_block(w_all, dest, width)[:, :out_cols]
        return lax.dot_general(
            mixed, block, (((1,), (1,)), ((), ())), preferred_element_type=jnp.float32
        )

    output = scattered_sum(out_part, "ctx", "tp", width).astype(jnp.bfloat16)
    grads = pullback((d_mixed, adjoint))
    d_values = grads[0] + skip_gain[None, :, None] * d_mixed
    d_pre = grads[3] * jax.nn.sigmoid(pre_step)
    d_pairs = jnp.stack([grads[1], grads[2]], axis=2).reshape(rows, pair_cols)
    d_cat = jnp.concatenate(
        [
            d_values.reshape(rows, inner).astype(jnp.bfloat16),
            d_pairs.astype(jnp.bfloat16),
            d_pre.astype(jnp.bfloat16),
        ],
        axis=1,
    )

    def grad_part(dest):
        block = row_block(w_all, dest, width)[:, out_cols:]
        return lax.dot_general(
            d_cat, block, (((1,), (1,)), ((), ())), preferred_element_type=jnp.float32
        )

    grad = scattered_sum(grad_part, "ctx", "tp", width).astype(jnp.bfloat16)
    return (output, grad)


def solution(mesh):
    placed = (
        P("ctx", "tp"),
        P("ctx", "tp"),
        P("ctx", "tp"),
        P("ctx", "tp"),
        P("tp"),
        P("tp"),
        P("tp"),
        P("tp", "ctx"),
        P("ctx", "tp"),
    )
    return jax.shard_map(
        per_device,
        mesh=mesh,
        in_specs=placed,
        out_specs=(P("ctx", "tp"), P("ctx", "tp")),
        check_vma=False,
    )
```

```python
import jax
import jax.numpy as jnp
from jax import lax
from jax.sharding import PartitionSpec as P

HEADDIM = 64
STATE = 128
SPAN = 256


HIGH = lax.Precision.HIGHEST
RING = 4


def both_carries(decay, forward, backward, axis):
    devices, position = (lax.axis_size(axis), lax.axis_index(axis))
    heads = decay.shape[0]
    own_a = decay[:, None]
    own_s = forward.reshape(heads, -1)
    own_u = backward.reshape(heads, -1)
    size = own_s.shape[1]
    message = jnp.concatenate([own_s, own_u, jnp.broadcast_to(own_a, (heads, 128))], axis=1)
    got = lax.ppermute(message, axis, [(i, i ^ 1) for i in range(devices)])
    sib_s = got[:, :size]
    sib_u = got[:, size : 2 * size]
    sib_a = got[:, 2 * size : 2 * size + 1]
    second = (position & 1) != 0
    first_a = jnp.where(second, sib_a, own_a)
    first_s = jnp.where(second, sib_s, own_s)
    last_a = jnp.where(second, own_a, sib_a)
    last_s = jnp.where(second, own_s, sib_s)
    first_u = jnp.where(second, sib_u, own_u)
    last_u = jnp.where(second, own_u, sib_u)
    total_a = first_a * last_a
    total_m = jnp.where(second, first_u + first_a * last_u, last_a * first_s + last_s)
    before_a = jnp.ones_like(total_a)
    before_m = jnp.zeros_like(total_m)
    bit = 2
    while bit < devices:
        message = jnp.concatenate([total_m, jnp.broadcast_to(total_a, (heads, 128))], axis=1)
        got = lax.ppermute(message, axis, [(i, i ^ bit) for i in range(devices)])
        got_m = got[:, :size]
        got_a = got[:, size : size + 1]
        flag = ((position & bit) != 0) != second
        before_m = jnp.where(flag, before_a * got_m + before_m, before_m)
        before_a = jnp.where(flag, before_a * got_a, before_a)
        total_m = jnp.where(flag, total_a * got_m + total_m, got_a * total_m + got_m)
        total_a = total_a * got_a
        bit *= 2
    got = lax.ppermute(before_m, axis, [(i, i ^ 1) for i in range(devices)])
    state_in = jnp.where(second, first_a * got + first_s, before_m)
    adjoint = jnp.where(second, before_m, last_u + last_a * got)
    return state_in.reshape(forward.shape), adjoint.reshape(backward.shape)


def scattered_sum(partial, rows_axis, axis, width):
    chains, devices = (lax.axis_size(rows_axis), lax.axis_size(axis))
    chain, position = (lax.axis_index(rows_axis), lax.axis_index(axis))
    ring = RING if devices % RING == 0 else 1

    def label(t, turn):
        return t - t % ring + (t + turn) % ring

    def place(lab, turn):
        return lab - lab % ring + (lab - turn) % ring

    turn = chain % 2
    mine_label = label(position, turn)
    order = [place(lab, 1) for lab in range(devices)]
    rows = partial.shape[0]
    blocks = partial.reshape(rows, devices, width)
    blocks = jnp.where(turn == 1, blocks[:, order], blocks)
    bit = 1
    while bit < devices:
        count = blocks.shape[1]
        paired = blocks.reshape(rows, count // 2, 2, width)
        mine = (mine_label & bit) != 0
        keep = jnp.where(mine, paired[:, :, 1], paired[:, :, 0])
        send = jnp.where(mine, paired[:, :, 0], paired[:, :, 1])
        pairs = []
        for c in range(chains):
            for t in range(devices):
                partner = place(label(t, c % 2) ^ bit, c % 2)
                pairs.append((c * devices + t, c * devices + partner))
        blocks = keep + lax.ppermute(send, (rows_axis, axis), pairs)
        bit *= 2
    return blocks.reshape(rows, width)


def ssd_core(values, b_rows, c_rows, step_size, decay_rate, state):
    length, heads, head_dim = values.shape
    groups = b_rows.shape[1]
    per_group = heads // groups
    blocks = length // SPAN
    lower_mask = (jnp.arange(SPAN)[:, None] >= jnp.arange(SPAN)[None, :])[None]

    def blocked(array):
        return array.reshape((blocks, SPAN) + array.shape[1:])

    def ssd_advance(carry, item):
        value_blk, b_blk, c_blk, step_blk = item
        cums = jnp.cumsum(-step_blk * decay_rate[None, :], axis=0)
        diff = cums.T[:, :, None] - cums.T[:, None, :]
        weight = jnp.where(lower_mask, jnp.exp(jnp.where(lower_mask, diff, 0.0)), 0.0)
        scores = jnp.einsum("tgn,sgn->gts", c_blk, b_blk, precision=HIGH)
        scores = jnp.repeat(scores, per_group, axis=0)
        inputs = step_blk[:, :, None] * value_blk
        inside = jnp.einsum("hts,shp->thp", scores * weight, inputs, precision=HIGH)
        c_head = jnp.repeat(c_blk, per_group, axis=1)
        b_head = jnp.repeat(b_blk, per_group, axis=1)
        carried = jnp.exp(cums)[:, :, None] * jnp.einsum(
            "thn,hpn->thp", c_head, carry, precision=HIGH
        )
        tail = jnp.exp(cums[-1][None, :] - cums)
        fresh = jnp.einsum("shp,shn->hpn", tail[:, :, None] * inputs, b_head, precision=HIGH)
        carry = jnp.exp(cums[-1])[:, None, None] * carry + fresh
        return (carry, inside + carried)

    final, outputs = lax.scan(
        jax.checkpoint(ssd_advance),
        state,
        (blocked(values), blocked(b_rows), blocked(c_rows), blocked(step_size)),
    )
    return (outputs.reshape(length, heads, head_dim), final)


def local_states(values, b_rows, step_size, decay_rate):
    length, heads, head_dim = values.shape
    groups = b_rows.shape[1]
    per_group = heads // groups
    blocks = length // SPAN

    def blocked(array):
        return array.reshape((blocks, SPAN) + array.shape[1:])

    def local_advance(carry, item):
        value_blk, b_blk, step_blk = item
        cums = jnp.cumsum(-step_blk * decay_rate[None, :], axis=0)
        tail = jnp.exp(cums[-1][None, :] - cums)
        b_head = jnp.repeat(b_blk, per_group, axis=1)
        inputs = (tail * step_blk)[:, :, None] * value_blk
        fresh = jnp.einsum("shp,shn->hpn", inputs, b_head, precision=HIGH)
        return (jnp.exp(cums[-1])[:, None, None] * carry + fresh, None)

    start = jnp.zeros((heads, head_dim, STATE), jnp.float32)
    final, unused = lax.scan(
        local_advance, start, (blocked(values), blocked(b_rows), blocked(step_size))
    )
    return final


def local_adjoint(d_mixed, c_rows, step_size, decay_rate):
    length, heads, head_dim = d_mixed.shape
    groups = c_rows.shape[1]
    per_group = heads // groups
    blocks = length // SPAN

    def blocked(array):
        return array.reshape((blocks, SPAN) + array.shape[1:])

    def retreat(carry, item):
        grad_blk, c_blk, step_blk = item
        cums = jnp.cumsum(-step_blk * decay_rate[None, :], axis=0)
        c_head = jnp.repeat(c_blk, per_group, axis=1)
        weighted = jnp.exp(cums)[:, :, None] * grad_blk
        term = jnp.einsum("thp,thn->hpn", weighted, c_head, precision=HIGH)
        return (term + jnp.exp(cums[-1])[:, None, None] * carry, None)

    start = jnp.zeros((heads, head_dim, STATE), jnp.float32)
    final, unused = lax.scan(
        retreat, start, (blocked(d_mixed), blocked(c_rows), blocked(step_size)), reverse=True
    )
    return final


def doubled_rows(x, axis, order):
    devices, position = (lax.axis_size(axis), lax.axis_index(axis))
    for b in order:
        bit = 1 << b
        other = lax.ppermute(x, axis, [(i, i ^ bit) for i in range(devices)])
        low = (position & bit) == 0
        x = jnp.where(low, jnp.concatenate([x, other], 0), jnp.concatenate([other, x], 0))
    rows = x.shape[0] // devices
    x = x.reshape((2,) * len(order) + (rows,) + x.shape[1:])
    axes = [len(order) - 1 - order.index(b) for b in reversed(range(len(order)))]
    x = jnp.transpose(x, axes + list(range(len(order), x.ndim)))
    return x.reshape((devices * rows,) + x.shape[len(order) + 1 :])


def row_block(w, index, size):
    return lax.dynamic_slice_in_dim(w, index * size, size, axis=0)


def per_device(tokens, w_in, w_bc, w_dt, dt_bias, decay_rate, skip_gain, w_out, cotangent):
    devices = lax.axis_size("tp")
    rows, width = tokens.shape
    heads = decay_rate.shape[0]
    inner = w_in.shape[1]
    pair_cols = w_bc.shape[1]
    groups = pair_cols // (2 * STATE)
    out_cols = w_out.shape[0]
    w_all = lax.all_gather(
        jnp.concatenate([w_out.T, w_in, w_bc, w_dt], axis=1), "ctx", axis=0, tiled=True
    )
    bits = devices.bit_length() - 1
    pieces = doubled_rows(
        jnp.concatenate([tokens, cotangent], axis=1), "tp", list(reversed(range(bits)))
    )
    projected = None
    d_flat = None
    for k in range(devices):
        block = w_all[k * width : (k + 1) * width]
        piece = pieces[k * rows : (k + 1) * rows]
        term = jnp.dot(piece[:, :width], block[:, out_cols:], preferred_element_type=jnp.float32)
        projected = term if projected is None else projected + term
        term = jnp.dot(piece[:, width:], block[:, :out_cols], preferred_element_type=jnp.float32)
        d_flat = term if d_flat is None else d_flat + term
    values = projected[:, :inner].astype(jnp.bfloat16)
    pairs = projected[:, inner : inner + pair_cols].astype(jnp.bfloat16)
    pre_step = projected[:, inner + pair_cols :] + dt_bias[None, :]
    step_size = jax.nn.softplus(pre_step)
    value_f = values.astype(jnp.float32).reshape(rows, heads, HEADDIM)
    paired = pairs.astype(jnp.float32).reshape(rows, groups, 2, STATE)
    b_rows = paired[:, :, 0]
    c_rows = paired[:, :, 1]
    end_state = local_states(value_f, b_rows, step_size, decay_rate)
    decay_total = jnp.exp(-jnp.sum(step_size * decay_rate[None, :], axis=0))
    d_mixed = d_flat.reshape(rows, heads, HEADDIM)
    own_adjoint = local_adjoint(d_mixed, c_rows, step_size, decay_rate)
    state_in, adjoint = both_carries(decay_total, end_state, own_adjoint, "ctx")

    def with_state(vals, brows, crows, steps):
        return ssd_core(vals, brows, crows, steps, decay_rate, state_in)

    (core_out, core_end), pullback = jax.vjp(with_state, value_f, b_rows, c_rows, step_size)
    mixed = (
        (core_out + skip_gain[None, :, None] * value_f).reshape(rows, inner).astype(jnp.bfloat16)
    )

    partial_out = lax.dot_general(
        mixed, w_all[:, :out_cols], (((1,), (1,)), ((), ())), preferred_element_type=jnp.float32
    )
    output = scattered_sum(partial_out, "ctx", "tp", width).astype(jnp.bfloat16)
    grads = pullback((d_mixed, adjoint))
    d_values = grads[0] + skip_gain[None, :, None] * d_mixed
    d_pre = grads[3] * jax.nn.sigmoid(pre_step)
    d_pairs = jnp.stack([grads[1], grads[2]], axis=2).reshape(rows, pair_cols)
    d_cat = jnp.concatenate(
        [
            d_values.reshape(rows, inner).astype(jnp.bfloat16),
            d_pairs.astype(jnp.bfloat16),
            d_pre.astype(jnp.bfloat16),
        ],
        axis=1,
    )

    partial_grad = lax.dot_general(
        d_cat, w_all[:, out_cols:], (((1,), (1,)), ((), ())), preferred_element_type=jnp.float32
    )
    grad = scattered_sum(partial_grad, "ctx", "tp", width).astype(jnp.bfloat16)
    return (output, grad)


def solution(mesh):
    placed = (
        P("ctx", "tp"),
        P("ctx", "tp"),
        P("ctx", "tp"),
        P("ctx", "tp"),
        P("tp"),
        P("tp"),
        P("tp"),
        P("tp", "ctx"),
        P("ctx", "tp"),
    )
    return jax.shard_map(
        per_device,
        mesh=mesh,
        in_specs=placed,
        out_specs=(P("ctx", "tp"), P("ctx", "tp")),
        check_vma=False,
    )
```

```python
import jax
import jax.numpy as jnp
from jax import lax
from jax.sharding import PartitionSpec as P

HEADDIM = 64
STATE = 128
SPAN = 256


HIGH = lax.Precision.HIGHEST
RING = 4


def both_carries(decay, forward, backward, axis):
    devices, position = (lax.axis_size(axis), lax.axis_index(axis))
    heads = decay.shape[0]
    own_a = decay[:, None]
    own_s = forward.reshape(heads, -1)
    own_u = backward.reshape(heads, -1)
    size = own_s.shape[1]
    message = jnp.concatenate([own_s, own_u, jnp.broadcast_to(own_a, (heads, 128))], axis=1)
    got = lax.ppermute(message, axis, [(i, i ^ 1) for i in range(devices)])
    sib_s = got[:, :size]
    sib_u = got[:, size : 2 * size]
    sib_a = got[:, 2 * size : 2 * size + 1]
    second = (position & 1) != 0
    first_a = jnp.where(second, sib_a, own_a)
    first_s = jnp.where(second, sib_s, own_s)
    last_a = jnp.where(second, own_a, sib_a)
    last_s = jnp.where(second, own_s, sib_s)
    first_u = jnp.where(second, sib_u, own_u)
    last_u = jnp.where(second, own_u, sib_u)
    total_a = first_a * last_a
    total_m = jnp.where(second, first_u + first_a * last_u, last_a * first_s + last_s)
    before_a = jnp.ones_like(total_a)
    before_m = jnp.zeros_like(total_m)
    bit = 2
    while bit < devices:
        message = jnp.concatenate([total_m, jnp.broadcast_to(total_a, (heads, 128))], axis=1)
        got = lax.ppermute(message, axis, [(i, i ^ bit) for i in range(devices)])
        got_m = got[:, :size]
        got_a = got[:, size : size + 1]
        flag = ((position & bit) != 0) != second
        before_m = jnp.where(flag, before_a * got_m + before_m, before_m)
        before_a = jnp.where(flag, before_a * got_a, before_a)
        total_m = jnp.where(flag, total_a * got_m + total_m, got_a * total_m + got_m)
        total_a = total_a * got_a
        bit *= 2
    got = lax.ppermute(before_m, axis, [(i, i ^ 1) for i in range(devices)])
    state_in = jnp.where(second, first_a * got + first_s, before_m)
    adjoint = jnp.where(second, before_m, last_u + last_a * got)
    return state_in.reshape(forward.shape), adjoint.reshape(backward.shape)


def scattered_sum(partial, rows_axis, axis, width):
    chains, devices = (lax.axis_size(rows_axis), lax.axis_size(axis))
    chain, position = (lax.axis_index(rows_axis), lax.axis_index(axis))
    ring = RING if devices % RING == 0 else 1

    def label(t, turn):
        return t - t % ring + (t + turn) % ring

    def place(lab, turn):
        return lab - lab % ring + (lab - turn) % ring

    turn = chain % 2
    mine_label = label(position, turn)
    rows = partial.shape[0]
    grouped = partial.reshape(rows, devices // ring, ring, width)
    rolled = jnp.concatenate([grouped[:, :, ring - 1 :], grouped[:, :, : ring - 1]], axis=2)
    blocks = jnp.where(turn == 1, rolled, grouped).reshape(rows, devices, width)
    bit = 1
    while bit < devices:
        count = blocks.shape[1]
        paired = blocks.reshape(rows, count // 2, 2, width)
        mine = (mine_label & bit) != 0
        keep = jnp.where(mine, paired[:, :, 1], paired[:, :, 0])
        send = jnp.where(mine, paired[:, :, 0], paired[:, :, 1])
        pairs = []
        for c in range(chains):
            for t in range(devices):
                partner = place(label(t, c % 2) ^ bit, c % 2)
                pairs.append((c * devices + t, c * devices + partner))
        blocks = keep + lax.ppermute(send, (rows_axis, axis), pairs)
        bit *= 2
    return blocks.reshape(rows, width)


def ssd_core(values, b_rows, c_rows, step_size, decay_rate, state):
    length, heads, head_dim = values.shape
    groups = b_rows.shape[1]
    per_group = heads // groups
    blocks = length // SPAN
    lower_mask = (jnp.arange(SPAN)[:, None] >= jnp.arange(SPAN)[None, :])[None]

    def blocked(array):
        return array.reshape((blocks, SPAN) + array.shape[1:])

    def ssd_advance(carry, item):
        value_blk, b_blk, c_blk, step_blk = item
        cums = jnp.cumsum(-step_blk * decay_rate[None, :], axis=0)
        diff = cums.T[:, :, None] - cums.T[:, None, :]
        weight = jnp.where(lower_mask, jnp.exp(jnp.where(lower_mask, diff, 0.0)), 0.0)
        scores = jnp.einsum("tgn,sgn->gts", c_blk, b_blk, precision=HIGH)
        scores = jnp.repeat(scores, per_group, axis=0)
        inputs = step_blk[:, :, None] * value_blk
        inside = jnp.einsum("hts,shp->thp", scores * weight, inputs, precision=HIGH)
        c_head = jnp.repeat(c_blk, per_group, axis=1)
        b_head = jnp.repeat(b_blk, per_group, axis=1)
        carried = jnp.exp(cums)[:, :, None] * jnp.einsum(
            "thn,hpn->thp", c_head, carry, precision=HIGH
        )
        tail = jnp.exp(cums[-1][None, :] - cums)
        fresh = jnp.einsum("shp,shn->hpn", tail[:, :, None] * inputs, b_head, precision=HIGH)
        carry = jnp.exp(cums[-1])[:, None, None] * carry + fresh
        return (carry, inside + carried)

    final, outputs = lax.scan(
        jax.checkpoint(ssd_advance),
        state,
        (blocked(values), blocked(b_rows), blocked(c_rows), blocked(step_size)),
    )
    return (outputs.reshape(length, heads, head_dim), final)


def local_states(values, b_rows, step_size, decay_rate):
    length, heads, head_dim = values.shape
    groups = b_rows.shape[1]
    per_group = heads // groups
    blocks = length // SPAN

    def blocked(array):
        return array.reshape((blocks, SPAN) + array.shape[1:])

    def local_advance(carry, item):
        value_blk, b_blk, step_blk = item
        cums = jnp.cumsum(-step_blk * decay_rate[None, :], axis=0)
        tail = jnp.exp(cums[-1][None, :] - cums)
        b_head = jnp.repeat(b_blk, per_group, axis=1)
        inputs = (tail * step_blk)[:, :, None] * value_blk
        fresh = jnp.einsum("shp,shn->hpn", inputs, b_head, precision=HIGH)
        return (jnp.exp(cums[-1])[:, None, None] * carry + fresh, None)

    start = jnp.zeros((heads, head_dim, STATE), jnp.float32)
    final, unused = lax.scan(
        local_advance, start, (blocked(values), blocked(b_rows), blocked(step_size))
    )
    return final


def local_adjoint(d_mixed, c_rows, step_size, decay_rate):
    length, heads, head_dim = d_mixed.shape
    groups = c_rows.shape[1]
    per_group = heads // groups
    blocks = length // SPAN

    def blocked(array):
        return array.reshape((blocks, SPAN) + array.shape[1:])

    def retreat(carry, item):
        grad_blk, c_blk, step_blk = item
        cums = jnp.cumsum(-step_blk * decay_rate[None, :], axis=0)
        c_head = jnp.repeat(c_blk, per_group, axis=1)
        weighted = jnp.exp(cums)[:, :, None] * grad_blk
        term = jnp.einsum("thp,thn->hpn", weighted, c_head, precision=HIGH)
        return (term + jnp.exp(cums[-1])[:, None, None] * carry, None)

    start = jnp.zeros((heads, head_dim, STATE), jnp.float32)
    final, unused = lax.scan(
        retreat, start, (blocked(d_mixed), blocked(c_rows), blocked(step_size)), reverse=True
    )
    return final


def doubled_rows(x, axis, order):
    devices, position = (lax.axis_size(axis), lax.axis_index(axis))
    for b in order:
        bit = 1 << b
        other = lax.ppermute(x, axis, [(i, i ^ bit) for i in range(devices)])
        low = (position & bit) == 0
        x = jnp.where(low, jnp.concatenate([x, other], 0), jnp.concatenate([other, x], 0))
    rows = x.shape[0] // devices
    x = x.reshape((2,) * len(order) + (rows,) + x.shape[1:])
    axes = [len(order) - 1 - order.index(b) for b in reversed(range(len(order)))]
    x = jnp.transpose(x, axes + list(range(len(order), x.ndim)))
    return x.reshape((devices * rows,) + x.shape[len(order) + 1 :])


def row_block(w, index, size):
    return lax.dynamic_slice_in_dim(w, index * size, size, axis=0)


def per_device(tokens, w_in, w_bc, w_dt, dt_bias, decay_rate, skip_gain, w_out, cotangent):
    devices = lax.axis_size("tp")
    rows, width = tokens.shape
    heads = decay_rate.shape[0]
    inner = w_in.shape[1]
    pair_cols = w_bc.shape[1]
    groups = pair_cols // (2 * STATE)
    out_cols = w_out.shape[0]
    w_all = lax.all_gather(
        jnp.concatenate([w_out.T, w_in, w_bc, w_dt], axis=1), "ctx", axis=0, tiled=True
    )
    bits = devices.bit_length() - 1
    pieces = doubled_rows(
        jnp.concatenate([tokens, cotangent], axis=1), "tp", list(reversed(range(bits)))
    )
    projected = None
    d_flat = None
    for k in range(devices):
        block = w_all[k * width : (k + 1) * width]
        piece = pieces[k * rows : (k + 1) * rows]
        term = jnp.dot(piece[:, :width], block[:, out_cols:], preferred_element_type=jnp.float32)
        projected = term if projected is None else projected + term
        term = jnp.dot(piece[:, width:], block[:, :out_cols], preferred_element_type=jnp.float32)
        d_flat = term if d_flat is None else d_flat + term
    values = projected[:, :inner].astype(jnp.bfloat16)
    pairs = projected[:, inner : inner + pair_cols].astype(jnp.bfloat16)
    pre_step = projected[:, inner + pair_cols :] + dt_bias[None, :]
    step_size = jax.nn.softplus(pre_step)
    value_f = values.astype(jnp.float32).reshape(rows, heads, HEADDIM)
    paired = pairs.astype(jnp.float32).reshape(rows, groups, 2, STATE)
    b_rows = paired[:, :, 0]
    c_rows = paired[:, :, 1]
    end_state = local_states(value_f, b_rows, step_size, decay_rate)
    decay_total = jnp.exp(-jnp.sum(step_size * decay_rate[None, :], axis=0))
    d_mixed = d_flat.reshape(rows, heads, HEADDIM)
    own_adjoint = local_adjoint(d_mixed, c_rows, step_size, decay_rate)
    state_in, adjoint = both_carries(decay_total, end_state, own_adjoint, "ctx")

    def with_state(vals, brows, crows, steps):
        return ssd_core(vals, brows, crows, steps, decay_rate, state_in)

    (core_out, core_end), pullback = jax.vjp(with_state, value_f, b_rows, c_rows, step_size)
    mixed = (
        (core_out + skip_gain[None, :, None] * value_f).reshape(rows, inner).astype(jnp.bfloat16)
    )

    partial_out = lax.dot_general(
        mixed, w_all[:, :out_cols], (((1,), (1,)), ((), ())), preferred_element_type=jnp.float32
    )
    output = scattered_sum(partial_out, "ctx", "tp", width).astype(jnp.bfloat16)
    grads = pullback((d_mixed, adjoint))
    d_values = grads[0] + skip_gain[None, :, None] * d_mixed
    d_pre = grads[3] * jax.nn.sigmoid(pre_step)
    d_pairs = jnp.stack([grads[1], grads[2]], axis=2).reshape(rows, pair_cols)
    d_cat = jnp.concatenate(
        [
            d_values.reshape(rows, inner).astype(jnp.bfloat16),
            d_pairs.astype(jnp.bfloat16),
            d_pre.astype(jnp.bfloat16),
        ],
        axis=1,
    )

    partial_grad = lax.dot_general(
        d_cat, w_all[:, out_cols:], (((1,), (1,)), ((), ())), preferred_element_type=jnp.float32
    )
    grad = scattered_sum(partial_grad, "ctx", "tp", width).astype(jnp.bfloat16)
    return (output, grad)


def solution(mesh):
    placed = (
        P("ctx", "tp"),
        P("ctx", "tp"),
        P("ctx", "tp"),
        P("ctx", "tp"),
        P("tp"),
        P("tp"),
        P("tp"),
        P("tp", "ctx"),
        P("ctx", "tp"),
    )
    return jax.shard_map(
        per_device,
        mesh=mesh,
        in_specs=placed,
        out_specs=(P("ctx", "tp"), P("ctx", "tp")),
        check_vma=False,
    )
```

```python
import jax
import jax.numpy as jnp
from jax import lax
from jax.sharding import PartitionSpec as P

HEADDIM = 64
STATE = 128
SPAN = 256


HIGH = lax.Precision.HIGH
RING = 4


def both_carries(decay, forward, backward, axis):
    devices, position = (lax.axis_size(axis), lax.axis_index(axis))
    heads = decay.shape[0]
    own_a = decay[:, None]
    own_s = forward.reshape(heads, -1)
    own_u = backward.reshape(heads, -1)
    size = own_s.shape[1]
    message = jnp.concatenate([own_s, own_u, jnp.broadcast_to(own_a, (heads, 128))], axis=1)
    got = lax.ppermute(message, axis, [(i, i ^ 1) for i in range(devices)])
    sib_s = got[:, :size]
    sib_u = got[:, size : 2 * size]
    sib_a = got[:, 2 * size : 2 * size + 1]
    second = (position & 1) != 0
    first_a = jnp.where(second, sib_a, own_a)
    first_s = jnp.where(second, sib_s, own_s)
    last_a = jnp.where(second, own_a, sib_a)
    last_s = jnp.where(second, own_s, sib_s)
    first_u = jnp.where(second, sib_u, own_u)
    last_u = jnp.where(second, own_u, sib_u)
    total_a = first_a * last_a
    total_m = jnp.where(second, first_u + first_a * last_u, last_a * first_s + last_s)
    before_a = jnp.ones_like(total_a)
    before_m = jnp.zeros_like(total_m)
    bit = 2
    while bit < devices:
        message = jnp.concatenate([total_m, jnp.broadcast_to(total_a, (heads, 128))], axis=1)
        got = lax.ppermute(message, axis, [(i, i ^ bit) for i in range(devices)])
        got_m = got[:, :size]
        got_a = got[:, size : size + 1]
        flag = ((position & bit) != 0) != second
        before_m = jnp.where(flag, before_a * got_m + before_m, before_m)
        before_a = jnp.where(flag, before_a * got_a, before_a)
        total_m = jnp.where(flag, total_a * got_m + total_m, got_a * total_m + got_m)
        total_a = total_a * got_a
        bit *= 2
    got = lax.ppermute(before_m, axis, [(i, i ^ 1) for i in range(devices)])
    state_in = jnp.where(second, first_a * got + first_s, before_m)
    adjoint = jnp.where(second, before_m, last_u + last_a * got)
    return state_in.reshape(forward.shape), adjoint.reshape(backward.shape)


def scattered_sum(partial, rows_axis, axis, width):
    chains, devices = (lax.axis_size(rows_axis), lax.axis_size(axis))
    chain, position = (lax.axis_index(rows_axis), lax.axis_index(axis))
    ring = RING if devices % RING == 0 else 1

    def label(t, turn):
        return t - t % ring + (t + turn) % ring

    def place(lab, turn):
        return lab - lab % ring + (lab - turn) % ring

    turn = chain % 2
    mine_label = label(position, turn)
    order = [place(lab, 1) for lab in range(devices)]
    rows = partial.shape[0]
    blocks = partial.reshape(rows, devices, width)
    blocks = jnp.where(turn == 1, blocks[:, order], blocks)
    bit = 1
    while bit < devices:
        count = blocks.shape[1]
        paired = blocks.reshape(rows, count // 2, 2, width)
        mine = (mine_label & bit) != 0
        keep = jnp.where(mine, paired[:, :, 1], paired[:, :, 0])
        send = jnp.where(mine, paired[:, :, 0], paired[:, :, 1])
        pairs = []
        for c in range(chains):
            for t in range(devices):
                partner = place(label(t, c % 2) ^ bit, c % 2)
                pairs.append((c * devices + t, c * devices + partner))
        blocks = keep + lax.ppermute(send, (rows_axis, axis), pairs)
        bit *= 2
    return blocks.reshape(rows, width)


def ssd_core(values, b_rows, c_rows, step_size, decay_rate, state):
    length, heads, head_dim = values.shape
    groups = b_rows.shape[1]
    per_group = heads // groups
    blocks = length // SPAN
    lower_mask = (jnp.arange(SPAN)[:, None] >= jnp.arange(SPAN)[None, :])[None]

    def blocked(array):
        return array.reshape((blocks, SPAN) + array.shape[1:])

    def ssd_advance(carry, item):
        value_blk, b_blk, c_blk, step_blk = item
        cums = jnp.cumsum(-step_blk * decay_rate[None, :], axis=0)
        diff = cums.T[:, :, None] - cums.T[:, None, :]
        weight = jnp.where(lower_mask, jnp.exp(jnp.where(lower_mask, diff, 0.0)), 0.0)
        scores = jnp.einsum("tgn,sgn->gts", c_blk, b_blk, precision=HIGH)
        scores = jnp.repeat(scores, per_group, axis=0)
        inputs = step_blk[:, :, None] * value_blk
        inside = jnp.einsum("hts,shp->thp", scores * weight, inputs, precision=HIGH)
        c_head = jnp.repeat(c_blk, per_group, axis=1)
        b_head = jnp.repeat(b_blk, per_group, axis=1)
        carried = jnp.exp(cums)[:, :, None] * jnp.einsum(
            "thn,hpn->thp", c_head, carry, precision=HIGH
        )
        tail = jnp.exp(cums[-1][None, :] - cums)
        fresh = jnp.einsum("shp,shn->hpn", tail[:, :, None] * inputs, b_head, precision=HIGH)
        carry = jnp.exp(cums[-1])[:, None, None] * carry + fresh
        return (carry, inside + carried)

    final, outputs = lax.scan(
        jax.checkpoint(ssd_advance),
        state,
        (blocked(values), blocked(b_rows), blocked(c_rows), blocked(step_size)),
    )
    return (outputs.reshape(length, heads, head_dim), final)


def local_states(values, b_rows, step_size, decay_rate):
    length, heads, head_dim = values.shape
    groups = b_rows.shape[1]
    per_group = heads // groups
    blocks = length // SPAN

    def blocked(array):
        return array.reshape((blocks, SPAN) + array.shape[1:])

    def local_advance(carry, item):
        value_blk, b_blk, step_blk = item
        cums = jnp.cumsum(-step_blk * decay_rate[None, :], axis=0)
        tail = jnp.exp(cums[-1][None, :] - cums)
        b_head = jnp.repeat(b_blk, per_group, axis=1)
        inputs = (tail * step_blk)[:, :, None] * value_blk
        fresh = jnp.einsum("shp,shn->hpn", inputs, b_head, precision=HIGH)
        return (jnp.exp(cums[-1])[:, None, None] * carry + fresh, None)

    start = jnp.zeros((heads, head_dim, STATE), jnp.float32)
    final, unused = lax.scan(
        local_advance, start, (blocked(values), blocked(b_rows), blocked(step_size))
    )
    return final


def local_adjoint(d_mixed, c_rows, step_size, decay_rate):
    length, heads, head_dim = d_mixed.shape
    groups = c_rows.shape[1]
    per_group = heads // groups
    blocks = length // SPAN

    def blocked(array):
        return array.reshape((blocks, SPAN) + array.shape[1:])

    def retreat(carry, item):
        grad_blk, c_blk, step_blk = item
        cums = jnp.cumsum(-step_blk * decay_rate[None, :], axis=0)
        c_head = jnp.repeat(c_blk, per_group, axis=1)
        weighted = jnp.exp(cums)[:, :, None] * grad_blk
        term = jnp.einsum("thp,thn->hpn", weighted, c_head, precision=HIGH)
        return (term + jnp.exp(cums[-1])[:, None, None] * carry, None)

    start = jnp.zeros((heads, head_dim, STATE), jnp.float32)
    final, unused = lax.scan(
        retreat, start, (blocked(d_mixed), blocked(c_rows), blocked(step_size)), reverse=True
    )
    return final


def doubled_rows(x, axis, order):
    devices, position = (lax.axis_size(axis), lax.axis_index(axis))
    for b in order:
        bit = 1 << b
        other = lax.ppermute(x, axis, [(i, i ^ bit) for i in range(devices)])
        low = (position & bit) == 0
        x = jnp.where(low, jnp.concatenate([x, other], 0), jnp.concatenate([other, x], 0))
    rows = x.shape[0] // devices
    x = x.reshape((2,) * len(order) + (rows,) + x.shape[1:])
    axes = [len(order) - 1 - order.index(b) for b in reversed(range(len(order)))]
    x = jnp.transpose(x, axes + list(range(len(order), x.ndim)))
    return x.reshape((devices * rows,) + x.shape[len(order) + 1 :])


def row_block(w, index, size):
    return lax.dynamic_slice_in_dim(w, index * size, size, axis=0)


def per_device(tokens, w_in, w_bc, w_dt, dt_bias, decay_rate, skip_gain, w_out, cotangent):
    devices = lax.axis_size("tp")
    rows, width = tokens.shape
    heads = decay_rate.shape[0]
    inner = w_in.shape[1]
    pair_cols = w_bc.shape[1]
    groups = pair_cols // (2 * STATE)
    out_cols = w_out.shape[0]
    w_all = lax.all_gather(
        jnp.concatenate([w_out.T, w_in, w_bc, w_dt], axis=1), "ctx", axis=0, tiled=True
    )
    bits = devices.bit_length() - 1
    pieces = doubled_rows(
        jnp.concatenate([tokens, cotangent], axis=1), "tp", list(reversed(range(bits)))
    )
    projected = None
    d_flat = None
    for k in range(devices):
        block = w_all[k * width : (k + 1) * width]
        piece = pieces[k * rows : (k + 1) * rows]
        term = jnp.dot(piece[:, :width], block[:, out_cols:], preferred_element_type=jnp.float32)
        projected = term if projected is None else projected + term
        term = jnp.dot(piece[:, width:], block[:, :out_cols], preferred_element_type=jnp.float32)
        d_flat = term if d_flat is None else d_flat + term
    values = projected[:, :inner].astype(jnp.bfloat16)
    pairs = projected[:, inner : inner + pair_cols].astype(jnp.bfloat16)
    pre_step = projected[:, inner + pair_cols :] + dt_bias[None, :]
    step_size = jax.nn.softplus(pre_step)
    value_f = values.astype(jnp.float32).reshape(rows, heads, HEADDIM)
    paired = pairs.astype(jnp.float32).reshape(rows, groups, 2, STATE)
    b_rows = paired[:, :, 0]
    c_rows = paired[:, :, 1]
    end_state = local_states(value_f, b_rows, step_size, decay_rate)
    decay_total = jnp.exp(-jnp.sum(step_size * decay_rate[None, :], axis=0))
    d_mixed = d_flat.reshape(rows, heads, HEADDIM)
    own_adjoint = local_adjoint(d_mixed, c_rows, step_size, decay_rate)
    state_in, adjoint = both_carries(decay_total, end_state, own_adjoint, "ctx")

    def with_state(vals, brows, crows, steps):
        return ssd_core(vals, brows, crows, steps, decay_rate, state_in)

    (core_out, core_end), pullback = jax.vjp(with_state, value_f, b_rows, c_rows, step_size)
    mixed = (
        (core_out + skip_gain[None, :, None] * value_f).reshape(rows, inner).astype(jnp.bfloat16)
    )

    partial_out = lax.dot_general(
        mixed, w_all[:, :out_cols], (((1,), (1,)), ((), ())), preferred_element_type=jnp.float32
    )
    output = scattered_sum(partial_out, "ctx", "tp", width).astype(jnp.bfloat16)
    grads = pullback((d_mixed, adjoint))
    d_values = grads[0] + skip_gain[None, :, None] * d_mixed
    d_pre = grads[3] * jax.nn.sigmoid(pre_step)
    d_pairs = jnp.stack([grads[1], grads[2]], axis=2).reshape(rows, pair_cols)
    d_cat = jnp.concatenate(
        [
            d_values.reshape(rows, inner).astype(jnp.bfloat16),
            d_pairs.astype(jnp.bfloat16),
            d_pre.astype(jnp.bfloat16),
        ],
        axis=1,
    )

    partial_grad = lax.dot_general(
        d_cat, w_all[:, out_cols:], (((1,), (1,)), ((), ())), preferred_element_type=jnp.float32
    )
    grad = scattered_sum(partial_grad, "ctx", "tp", width).astype(jnp.bfloat16)
    return (output, grad)


def solution(mesh):
    placed = (
        P("ctx", "tp"),
        P("ctx", "tp"),
        P("ctx", "tp"),
        P("ctx", "tp"),
        P("tp"),
        P("tp"),
        P("tp"),
        P("tp", "ctx"),
        P("ctx", "tp"),
    )
    return jax.shard_map(
        per_device,
        mesh=mesh,
        in_specs=placed,
        out_specs=(P("ctx", "tp"), P("ctx", "tp")),
        check_vma=False,
    )
```

```python
import jax
import jax.numpy as jnp
from jax import lax
from jax.sharding import PartitionSpec as P

HEADDIM = 64
STATE = 128
SPAN = 256


HIGH = lax.Precision.HIGH
RING = 4


def both_carries(decay, forward, backward, axis):
    devices, position = (lax.axis_size(axis), lax.axis_index(axis))
    heads = decay.shape[0]
    own_a = decay[:, None]
    own_s = forward.reshape(heads, -1)
    own_u = backward.reshape(heads, -1)
    size = own_s.shape[1]
    message = jnp.concatenate([own_s, own_u, jnp.broadcast_to(own_a, (heads, 128))], axis=1)
    got = lax.ppermute(message, axis, [(i, i ^ 1) for i in range(devices)])
    sib_s = got[:, :size]
    sib_u = got[:, size : 2 * size]
    sib_a = got[:, 2 * size : 2 * size + 1]
    second = (position & 1) != 0
    first_a = jnp.where(second, sib_a, own_a)
    first_s = jnp.where(second, sib_s, own_s)
    last_a = jnp.where(second, own_a, sib_a)
    last_s = jnp.where(second, own_s, sib_s)
    first_u = jnp.where(second, sib_u, own_u)
    last_u = jnp.where(second, own_u, sib_u)
    total_a = first_a * last_a
    total_m = jnp.where(second, first_u + first_a * last_u, last_a * first_s + last_s)
    before_a = jnp.ones_like(total_a)
    before_m = jnp.zeros_like(total_m)
    bit = 2
    while bit < devices:
        message = jnp.concatenate([total_m, jnp.broadcast_to(total_a, (heads, 128))], axis=1)
        got = lax.ppermute(message, axis, [(i, i ^ bit) for i in range(devices)])
        got_m = got[:, :size]
        got_a = got[:, size : size + 1]
        flag = ((position & bit) != 0) != second
        before_m = jnp.where(flag, before_a * got_m + before_m, before_m)
        before_a = jnp.where(flag, before_a * got_a, before_a)
        total_m = jnp.where(flag, total_a * got_m + total_m, got_a * total_m + got_m)
        total_a = total_a * got_a
        bit *= 2
    got = lax.ppermute(before_m, axis, [(i, i ^ 1) for i in range(devices)])
    state_in = jnp.where(second, first_a * got + first_s, before_m)
    adjoint = jnp.where(second, before_m, last_u + last_a * got)
    return state_in.reshape(forward.shape), adjoint.reshape(backward.shape)


def scattered_sum(partial, rows_axis, axis, width):
    chains, devices = (lax.axis_size(rows_axis), lax.axis_size(axis))
    chain, position = (lax.axis_index(rows_axis), lax.axis_index(axis))
    ring = RING if devices % RING == 0 else 1

    def label(t, turn):
        return t - t % ring + (t + turn) % ring

    def place(lab, turn):
        return lab - lab % ring + (lab - turn) % ring

    turn = chain % 2
    mine_label = label(position, turn)
    order = [place(lab, 1) for lab in range(devices)]
    rows = partial.shape[0]
    blocks = partial.reshape(rows, devices, width)
    blocks = jnp.where(turn == 1, blocks[:, order], blocks)
    bit = 1
    while bit < devices:
        count = blocks.shape[1]
        paired = blocks.reshape(rows, count // 2, 2, width)
        mine = (mine_label & bit) != 0
        keep = jnp.where(mine, paired[:, :, 1], paired[:, :, 0])
        send = jnp.where(mine, paired[:, :, 0], paired[:, :, 1])
        pairs = []
        for c in range(chains):
            for t in range(devices):
                partner = place(label(t, c % 2) ^ bit, c % 2)
                pairs.append((c * devices + t, c * devices + partner))
        blocks = keep + lax.ppermute(send, (rows_axis, axis), pairs)
        bit *= 2
    return blocks.reshape(rows, width)


def ssd_core(values, b_rows, c_rows, step_size, decay_rate, state):
    length, heads, head_dim = values.shape
    groups = b_rows.shape[1]
    per_group = heads // groups
    blocks = length // SPAN
    lower_mask = (jnp.arange(SPAN)[:, None] >= jnp.arange(SPAN)[None, :])[None]

    def blocked(array):
        return array.reshape((blocks, SPAN) + array.shape[1:])

    def ssd_advance(carry, item):
        value_blk, b_blk, c_blk, step_blk = item
        cums = jnp.cumsum(-step_blk * decay_rate[None, :], axis=0)
        diff = cums.T[:, :, None] - cums.T[:, None, :]
        weight = jnp.where(lower_mask, jnp.exp(jnp.where(lower_mask, diff, 0.0)), 0.0)
        scores = jnp.einsum("tgn,sgn->gts", c_blk, b_blk, precision=HIGH)
        scores = jnp.repeat(scores, per_group, axis=0)
        inputs = step_blk[:, :, None] * value_blk
        inside = jnp.einsum("hts,shp->thp", scores * weight, inputs, precision=HIGH)
        c_head = jnp.repeat(c_blk, per_group, axis=1)
        b_head = jnp.repeat(b_blk, per_group, axis=1)
        carried = jnp.exp(cums)[:, :, None] * jnp.einsum(
            "thn,hpn->thp", c_head, carry, precision=HIGH
        )
        tail = jnp.exp(cums[-1][None, :] - cums)
        fresh = jnp.einsum("shp,shn->hpn", tail[:, :, None] * inputs, b_head, precision=HIGH)
        carry = jnp.exp(cums[-1])[:, None, None] * carry + fresh
        return (carry, inside + carried)

    final, outputs = lax.scan(
        jax.checkpoint(ssd_advance),
        state,
        (blocked(values), blocked(b_rows), blocked(c_rows), blocked(step_size)),
    )
    return (outputs.reshape(length, heads, head_dim), final)


def local_states(values, b_rows, step_size, decay_rate):
    length, heads, head_dim = values.shape
    groups = b_rows.shape[1]
    per_group = heads // groups
    blocks = length // SPAN

    def blocked(array):
        return array.reshape((blocks, SPAN) + array.shape[1:])

    def local_advance(carry, item):
        value_blk, b_blk, step_blk = item
        cums = jnp.cumsum(-step_blk * decay_rate[None, :], axis=0)
        tail = jnp.exp(cums[-1][None, :] - cums)
        b_head = jnp.repeat(b_blk, per_group, axis=1)
        inputs = (tail * step_blk)[:, :, None] * value_blk
        fresh = jnp.einsum("shp,shn->hpn", inputs, b_head, precision=HIGH)
        return (jnp.exp(cums[-1])[:, None, None] * carry + fresh, None)

    start = jnp.zeros((heads, head_dim, STATE), jnp.float32)
    final, unused = lax.scan(
        local_advance, start, (blocked(values), blocked(b_rows), blocked(step_size))
    )
    return final


def local_adjoint(d_mixed, c_rows, step_size, decay_rate):
    length, heads, head_dim = d_mixed.shape
    groups = c_rows.shape[1]
    per_group = heads // groups
    blocks = length // SPAN

    def blocked(array):
        return array.reshape((blocks, SPAN) + array.shape[1:])

    def retreat(carry, item):
        grad_blk, c_blk, step_blk = item
        cums = jnp.cumsum(-step_blk * decay_rate[None, :], axis=0)
        c_head = jnp.repeat(c_blk, per_group, axis=1)
        weighted = jnp.exp(cums)[:, :, None] * grad_blk
        term = jnp.einsum("thp,thn->hpn", weighted, c_head, precision=HIGH)
        return (term + jnp.exp(cums[-1])[:, None, None] * carry, None)

    start = jnp.zeros((heads, head_dim, STATE), jnp.float32)
    final, unused = lax.scan(
        retreat, start, (blocked(d_mixed), blocked(c_rows), blocked(step_size)), reverse=True
    )
    return final


def doubled_rows(x, axis, order):
    devices, position = (lax.axis_size(axis), lax.axis_index(axis))
    for b in order:
        bit = 1 << b
        other = lax.ppermute(x, axis, [(i, i ^ bit) for i in range(devices)])
        low = (position & bit) == 0
        x = jnp.where(low, jnp.concatenate([x, other], 0), jnp.concatenate([other, x], 0))
    rows = x.shape[0] // devices
    x = x.reshape((2,) * len(order) + (rows,) + x.shape[1:])
    axes = [len(order) - 1 - order.index(b) for b in reversed(range(len(order)))]
    x = jnp.transpose(x, axes + list(range(len(order), x.ndim)))
    return x.reshape((devices * rows,) + x.shape[len(order) + 1 :])


def row_block(w, index, size):
    return lax.dynamic_slice_in_dim(w, index * size, size, axis=0)


def per_device(tokens, w_in, w_bc, w_dt, dt_bias, decay_rate, skip_gain, w_out, cotangent):
    devices = lax.axis_size("tp")
    rows, width = tokens.shape
    heads = decay_rate.shape[0]
    inner = w_in.shape[1]
    pair_cols = w_bc.shape[1]
    groups = pair_cols // (2 * STATE)
    out_cols = w_out.shape[0]
    w_own = jnp.concatenate([w_out.T, w_in, w_bc, w_dt], axis=1)
    lanes = 128 if w_own.size % 128 == 0 else w_own.shape[1]
    w_all = lax.all_gather(
        w_own.reshape(-1, lanes), "ctx", axis=0, tiled=True
    ).reshape(-1, w_own.shape[1])
    bits = devices.bit_length() - 1
    pieces = doubled_rows(
        jnp.concatenate([tokens, cotangent], axis=1), "tp", list(reversed(range(bits)))
    )
    projected = None
    d_flat = None
    for k in range(devices):
        block = w_all[k * width : (k + 1) * width]
        piece = pieces[k * rows : (k + 1) * rows]
        term = jnp.dot(piece[:, :width], block[:, out_cols:], preferred_element_type=jnp.float32)
        projected = term if projected is None else projected + term
        term = jnp.dot(piece[:, width:], block[:, :out_cols], preferred_element_type=jnp.float32)
        d_flat = term if d_flat is None else d_flat + term
    values = projected[:, :inner].astype(jnp.bfloat16)
    pairs = projected[:, inner : inner + pair_cols].astype(jnp.bfloat16)
    pre_step = projected[:, inner + pair_cols :] + dt_bias[None, :]
    step_size = jax.nn.softplus(pre_step)
    value_f = values.astype(jnp.float32).reshape(rows, heads, HEADDIM)
    paired = pairs.astype(jnp.float32).reshape(rows, groups, 2, STATE)
    b_rows = paired[:, :, 0]
    c_rows = paired[:, :, 1]
    end_state = local_states(value_f, b_rows, step_size, decay_rate)
    decay_total = jnp.exp(-jnp.sum(step_size * decay_rate[None, :], axis=0))
    d_mixed = d_flat.reshape(rows, heads, HEADDIM)
    own_adjoint = local_adjoint(d_mixed, c_rows, step_size, decay_rate)
    state_in, adjoint = both_carries(decay_total, end_state, own_adjoint, "ctx")

    def with_state(vals, brows, crows, steps):
        return ssd_core(vals, brows, crows, steps, decay_rate, state_in)

    (core_out, core_end), pullback = jax.vjp(with_state, value_f, b_rows, c_rows, step_size)
    mixed = (
        (core_out + skip_gain[None, :, None] * value_f).reshape(rows, inner).astype(jnp.bfloat16)
    )

    partial_out = lax.dot_general(
        mixed, w_all[:, :out_cols], (((1,), (1,)), ((), ())), preferred_element_type=jnp.float32
    )
    output = scattered_sum(partial_out, "ctx", "tp", width).astype(jnp.bfloat16)
    grads = pullback((d_mixed, adjoint))
    d_values = grads[0] + skip_gain[None, :, None] * d_mixed
    d_pre = grads[3] * jax.nn.sigmoid(pre_step)
    d_pairs = jnp.stack([grads[1], grads[2]], axis=2).reshape(rows, pair_cols)
    d_cat = jnp.concatenate(
        [
            d_values.reshape(rows, inner).astype(jnp.bfloat16),
            d_pairs.astype(jnp.bfloat16),
            d_pre.astype(jnp.bfloat16),
        ],
        axis=1,
    )

    partial_grad = lax.dot_general(
        d_cat, w_all[:, out_cols:], (((1,), (1,)), ((), ())), preferred_element_type=jnp.float32
    )
    grad = scattered_sum(partial_grad, "ctx", "tp", width).astype(jnp.bfloat16)
    return (output, grad)


def solution(mesh):
    placed = (
        P("ctx", "tp"),
        P("ctx", "tp"),
        P("ctx", "tp"),
        P("ctx", "tp"),
        P("tp"),
        P("tp"),
        P("tp"),
        P("tp", "ctx"),
        P("ctx", "tp"),
    )
    return jax.shard_map(
        per_device,
        mesh=mesh,
        in_specs=placed,
        out_specs=(P("ctx", "tp"), P("ctx", "tp")),
        check_vma=False,
    )
```

```python
import jax
import jax.numpy as jnp
from jax import lax
from jax.sharding import PartitionSpec as P

HEADDIM = 64
STATE = 128
SPAN = 256


HIGH = lax.Precision.HIGH
RING = 4


def both_carries(decay, forward, backward, axis):
    devices, position = (lax.axis_size(axis), lax.axis_index(axis))
    heads = decay.shape[0]
    own_a = decay[:, None]
    own_s = forward.reshape(heads, -1)
    own_u = backward.reshape(heads, -1)
    size = own_s.shape[1]
    message = jnp.concatenate([own_s, own_u, jnp.broadcast_to(own_a, (heads, 128))], axis=1)
    got = lax.ppermute(message, axis, [(i, i ^ 1) for i in range(devices)])
    sib_s = got[:, :size]
    sib_u = got[:, size : 2 * size]
    sib_a = got[:, 2 * size : 2 * size + 1]
    second = (position & 1) != 0
    first_a = jnp.where(second, sib_a, own_a)
    first_s = jnp.where(second, sib_s, own_s)
    last_a = jnp.where(second, own_a, sib_a)
    last_s = jnp.where(second, own_s, sib_s)
    first_u = jnp.where(second, sib_u, own_u)
    last_u = jnp.where(second, own_u, sib_u)
    total_a = first_a * last_a
    total_m = jnp.where(second, first_u + first_a * last_u, last_a * first_s + last_s)
    before_a = jnp.ones_like(total_a)
    before_m = jnp.zeros_like(total_m)
    bit = 2
    while bit < devices:
        message = jnp.concatenate([total_m, jnp.broadcast_to(total_a, (heads, 128))], axis=1)
        got = lax.ppermute(message, axis, [(i, i ^ bit) for i in range(devices)])
        got_m = got[:, :size]
        got_a = got[:, size : size + 1]
        flag = ((position & bit) != 0) != second
        before_m = jnp.where(flag, before_a * got_m + before_m, before_m)
        before_a = jnp.where(flag, before_a * got_a, before_a)
        total_m = jnp.where(flag, total_a * got_m + total_m, got_a * total_m + got_m)
        total_a = total_a * got_a
        bit *= 2
    got = lax.ppermute(before_m, axis, [(i, i ^ 1) for i in range(devices)])
    state_in = jnp.where(second, first_a * got + first_s, before_m)
    adjoint = jnp.where(second, before_m, last_u + last_a * got)
    return state_in.reshape(forward.shape), adjoint.reshape(backward.shape)


def scattered_sum(partial, rows_axis, axis, width):
    chains, devices = (lax.axis_size(rows_axis), lax.axis_size(axis))
    chain, position = (lax.axis_index(rows_axis), lax.axis_index(axis))
    ring = RING if devices % RING == 0 else 1

    def label(t, turn):
        return t - t % ring + (t + turn) % ring

    def place(lab, turn):
        return lab - lab % ring + (lab - turn) % ring

    turn = chain % 2
    mine_label = label(position, turn)
    order = [place(lab, 1) for lab in range(devices)]
    rows = partial.shape[0]
    blocks = partial.reshape(rows, devices, width)
    blocks = jnp.where(turn == 1, blocks[:, order], blocks)
    bit = 1
    while bit < devices:
        count = blocks.shape[1]
        paired = blocks.reshape(rows, count // 2, 2, width)
        mine = (mine_label & bit) != 0
        keep = jnp.where(mine, paired[:, :, 1], paired[:, :, 0])
        send = jnp.where(mine, paired[:, :, 0], paired[:, :, 1])
        pairs = []
        for c in range(chains):
            for t in range(devices):
                partner = place(label(t, c % 2) ^ bit, c % 2)
                pairs.append((c * devices + t, c * devices + partner))
        blocks = keep + lax.ppermute(send, (rows_axis, axis), pairs)
        bit *= 2
    return blocks.reshape(rows, width)


def ssd_core(values, b_rows, c_rows, step_size, decay_rate, state):
    length, heads, head_dim = values.shape
    groups = b_rows.shape[1]
    per_group = heads // groups
    blocks = length // SPAN
    lower_mask = (jnp.arange(SPAN)[:, None] >= jnp.arange(SPAN)[None, :])[None]

    def blocked(array):
        return array.reshape((blocks, SPAN) + array.shape[1:])

    def ssd_advance(carry, item):
        value_blk, b_blk, c_blk, step_blk = item
        cums = jnp.cumsum(-step_blk * decay_rate[None, :], axis=0)
        diff = cums.T[:, :, None] - cums.T[:, None, :]
        weight = jnp.where(lower_mask, jnp.exp(jnp.where(lower_mask, diff, 0.0)), 0.0)
        scores = jnp.einsum("tgn,sgn->gts", c_blk, b_blk, precision=HIGH)
        scores = jnp.repeat(scores, per_group, axis=0)
        inputs = step_blk[:, :, None] * value_blk
        inside = jnp.einsum("hts,shp->thp", scores * weight, inputs, precision=HIGH)
        c_head = jnp.repeat(c_blk, per_group, axis=1)
        b_head = jnp.repeat(b_blk, per_group, axis=1)
        carried = jnp.exp(cums)[:, :, None] * jnp.einsum(
            "thn,hpn->thp", c_head, carry, precision=HIGH
        )
        tail = jnp.exp(cums[-1][None, :] - cums)
        fresh = jnp.einsum("shp,shn->hpn", tail[:, :, None] * inputs, b_head, precision=HIGH)
        carry = jnp.exp(cums[-1])[:, None, None] * carry + fresh
        return (carry, inside + carried)

    final, outputs = lax.scan(
        jax.checkpoint(ssd_advance),
        state,
        (blocked(values), blocked(b_rows), blocked(c_rows), blocked(step_size)),
    )
    return (outputs.reshape(length, heads, head_dim), final)


def local_states(values, b_rows, step_size, decay_rate):
    length, heads, head_dim = values.shape
    groups = b_rows.shape[1]
    per_group = heads // groups
    blocks = length // SPAN

    def blocked(array):
        return array.reshape((blocks, SPAN) + array.shape[1:])

    def local_advance(carry, item):
        value_blk, b_blk, step_blk = item
        cums = jnp.cumsum(-step_blk * decay_rate[None, :], axis=0)
        tail = jnp.exp(cums[-1][None, :] - cums)
        b_head = jnp.repeat(b_blk, per_group, axis=1)
        inputs = (tail * step_blk)[:, :, None] * value_blk
        fresh = jnp.einsum("shp,shn->hpn", inputs, b_head, precision=HIGH)
        return (jnp.exp(cums[-1])[:, None, None] * carry + fresh, None)

    start = jnp.zeros((heads, head_dim, STATE), jnp.float32)
    final, unused = lax.scan(
        local_advance, start, (blocked(values), blocked(b_rows), blocked(step_size))
    )
    return final


def local_adjoint(d_mixed, c_rows, step_size, decay_rate):
    length, heads, head_dim = d_mixed.shape
    groups = c_rows.shape[1]
    per_group = heads // groups
    blocks = length // SPAN

    def blocked(array):
        return array.reshape((blocks, SPAN) + array.shape[1:])

    def retreat(carry, item):
        grad_blk, c_blk, step_blk = item
        cums = jnp.cumsum(-step_blk * decay_rate[None, :], axis=0)
        c_head = jnp.repeat(c_blk, per_group, axis=1)
        weighted = jnp.exp(cums)[:, :, None] * grad_blk
        term = jnp.einsum("thp,thn->hpn", weighted, c_head, precision=HIGH)
        return (term + jnp.exp(cums[-1])[:, None, None] * carry, None)

    start = jnp.zeros((heads, head_dim, STATE), jnp.float32)
    final, unused = lax.scan(
        retreat, start, (blocked(d_mixed), blocked(c_rows), blocked(step_size)), reverse=True
    )
    return final


def doubled_rows(x, axis, order):
    devices, position = (lax.axis_size(axis), lax.axis_index(axis))
    for b in order:
        bit = 1 << b
        other = lax.ppermute(x, axis, [(i, i ^ bit) for i in range(devices)])
        low = (position & bit) == 0
        x = jnp.where(low, jnp.concatenate([x, other], 0), jnp.concatenate([other, x], 0))
    rows = x.shape[0] // devices
    x = x.reshape((2,) * len(order) + (rows,) + x.shape[1:])
    axes = [len(order) - 1 - order.index(b) for b in reversed(range(len(order)))]
    x = jnp.transpose(x, axes + list(range(len(order), x.ndim)))
    return x.reshape((devices * rows,) + x.shape[len(order) + 1 :])


def row_block(w, index, size):
    return lax.dynamic_slice_in_dim(w, index * size, size, axis=0)


def per_device(tokens, w_in, w_bc, w_dt, dt_bias, decay_rate, skip_gain, w_out, cotangent):
    devices = lax.axis_size("tp")
    rows, width = tokens.shape
    heads = decay_rate.shape[0]
    inner = w_in.shape[1]
    pair_cols = w_bc.shape[1]
    groups = pair_cols // (2 * STATE)
    out_cols = w_out.shape[0]
    w_all = lax.all_gather(
        jnp.concatenate([w_out.T, w_in, w_bc, w_dt], axis=1), "ctx", axis=0, tiled=True
    )
    bits = devices.bit_length() - 1
    pieces = doubled_rows(
        jnp.concatenate([tokens, cotangent], axis=1), "tp", list(reversed(range(bits)))
    )
    stacked = pieces.reshape(devices, rows, 2 * width)
    w_blocks = w_all.reshape(devices, width, w_all.shape[1])
    both_dims = (((0, 2), (0, 1)), ((), ()))
    projected = lax.dot_general(
        stacked[:, :, :width], w_blocks[:, :, out_cols:], both_dims,
        preferred_element_type=jnp.float32,
    )
    d_flat = lax.dot_general(
        stacked[:, :, width:], w_blocks[:, :, :out_cols], both_dims,
        preferred_element_type=jnp.float32,
    )
    values = projected[:, :inner].astype(jnp.bfloat16)
    pairs = projected[:, inner : inner + pair_cols].astype(jnp.bfloat16)
    pre_step = projected[:, inner + pair_cols :] + dt_bias[None, :]
    step_size = jax.nn.softplus(pre_step)
    value_f = values.astype(jnp.float32).reshape(rows, heads, HEADDIM)
    paired = pairs.astype(jnp.float32).reshape(rows, groups, 2, STATE)
    b_rows = paired[:, :, 0]
    c_rows = paired[:, :, 1]
    end_state = local_states(value_f, b_rows, step_size, decay_rate)
    decay_total = jnp.exp(-jnp.sum(step_size * decay_rate[None, :], axis=0))
    d_mixed = d_flat.reshape(rows, heads, HEADDIM)
    own_adjoint = local_adjoint(d_mixed, c_rows, step_size, decay_rate)
    state_in, adjoint = both_carries(decay_total, end_state, own_adjoint, "ctx")

    def with_state(vals, brows, crows, steps):
        return ssd_core(vals, brows, crows, steps, decay_rate, state_in)

    (core_out, core_end), pullback = jax.vjp(with_state, value_f, b_rows, c_rows, step_size)
    mixed = (
        (core_out + skip_gain[None, :, None] * value_f).reshape(rows, inner).astype(jnp.bfloat16)
    )

    partial_out = lax.dot_general(
        mixed, w_all[:, :out_cols], (((1,), (1,)), ((), ())), preferred_element_type=jnp.float32
    )
    output = scattered_sum(partial_out, "ctx", "tp", width).astype(jnp.bfloat16)
    grads = pullback((d_mixed, adjoint))
    d_values = grads[0] + skip_gain[None, :, None] * d_mixed
    d_pre = grads[3] * jax.nn.sigmoid(pre_step)
    d_pairs = jnp.stack([grads[1], grads[2]], axis=2).reshape(rows, pair_cols)
    d_cat = jnp.concatenate(
        [
            d_values.reshape(rows, inner).astype(jnp.bfloat16),
            d_pairs.astype(jnp.bfloat16),
            d_pre.astype(jnp.bfloat16),
        ],
        axis=1,
    )

    partial_grad = lax.dot_general(
        d_cat, w_all[:, out_cols:], (((1,), (1,)), ((), ())), preferred_element_type=jnp.float32
    )
    grad = scattered_sum(partial_grad, "ctx", "tp", width).astype(jnp.bfloat16)
    return (output, grad)


def solution(mesh):
    placed = (
        P("ctx", "tp"),
        P("ctx", "tp"),
        P("ctx", "tp"),
        P("ctx", "tp"),
        P("tp"),
        P("tp"),
        P("tp"),
        P("tp", "ctx"),
        P("ctx", "tp"),
    )
    return jax.shard_map(
        per_device,
        mesh=mesh,
        in_specs=placed,
        out_specs=(P("ctx", "tp"), P("ctx", "tp")),
        check_vma=False,
    )
```

```python
import jax
import jax.numpy as jnp
from jax import lax
from jax.sharding import PartitionSpec as P

HEADDIM = 64
STATE = 128
SPAN = 256


HIGH = lax.Precision.HIGH
RING = 4


def both_carries(decay, forward, backward, axis):
    devices, position = (lax.axis_size(axis), lax.axis_index(axis))
    heads = decay.shape[0]
    own_a = decay[:, None]
    own_s = forward.reshape(heads, -1)
    own_u = backward.reshape(heads, -1)
    size = own_s.shape[1]
    message = jnp.concatenate([own_s, own_u, jnp.broadcast_to(own_a, (heads, 128))], axis=1)
    got = lax.ppermute(message, axis, [(i, i ^ 1) for i in range(devices)])
    sib_s = got[:, :size]
    sib_u = got[:, size : 2 * size]
    sib_a = got[:, 2 * size : 2 * size + 1]
    second = (position & 1) != 0
    first_a = jnp.where(second, sib_a, own_a)
    first_s = jnp.where(second, sib_s, own_s)
    last_a = jnp.where(second, own_a, sib_a)
    last_s = jnp.where(second, own_s, sib_s)
    first_u = jnp.where(second, sib_u, own_u)
    last_u = jnp.where(second, own_u, sib_u)
    total_a = first_a * last_a
    total_m = jnp.where(second, first_u + first_a * last_u, last_a * first_s + last_s)
    before_a = jnp.ones_like(total_a)
    before_m = jnp.zeros_like(total_m)
    bit = 2
    while bit < devices:
        if 2 * bit >= devices:
            wanted = [
                (i, i ^ bit) for i in range(devices) if ((i & bit) != 0) == ((i & 1) != 0)
            ]
            got_m = lax.ppermute(total_m, axis, wanted)
            flag = ((position & bit) != 0) != second
            before_m = jnp.where(flag, before_a * got_m + before_m, before_m)
            break
        message = jnp.concatenate([total_m, jnp.broadcast_to(total_a, (heads, 128))], axis=1)
        got = lax.ppermute(message, axis, [(i, i ^ bit) for i in range(devices)])
        got_m = got[:, :size]
        got_a = got[:, size : size + 1]
        flag = ((position & bit) != 0) != second
        before_m = jnp.where(flag, before_a * got_m + before_m, before_m)
        before_a = jnp.where(flag, before_a * got_a, before_a)
        total_m = jnp.where(flag, total_a * got_m + total_m, got_a * total_m + got_m)
        total_a = total_a * got_a
        bit *= 2
    got = lax.ppermute(before_m, axis, [(i, i ^ 1) for i in range(devices)])
    state_in = jnp.where(second, first_a * got + first_s, before_m)
    adjoint = jnp.where(second, before_m, last_u + last_a * got)
    return state_in.reshape(forward.shape), adjoint.reshape(backward.shape)


def scattered_sum(partial, rows_axis, axis, width):
    chains, devices = (lax.axis_size(rows_axis), lax.axis_size(axis))
    chain, position = (lax.axis_index(rows_axis), lax.axis_index(axis))
    ring = RING if devices % RING == 0 else 1

    def label(t, turn):
        return t - t % ring + (t + turn) % ring

    def place(lab, turn):
        return lab - lab % ring + (lab - turn) % ring

    turn = chain % 2
    mine_label = label(position, turn)
    order = [place(lab, 1) for lab in range(devices)]
    rows = partial.shape[0]
    blocks = partial.reshape(rows, devices, width)
    blocks = jnp.where(turn == 1, blocks[:, order], blocks)
    bit = 1
    while bit < devices:
        count = blocks.shape[1]
        paired = blocks.reshape(rows, count // 2, 2, width)
        mine = (mine_label & bit) != 0
        keep = jnp.where(mine, paired[:, :, 1], paired[:, :, 0])
        send = jnp.where(mine, paired[:, :, 0], paired[:, :, 1])
        pairs = []
        for c in range(chains):
            for t in range(devices):
                partner = place(label(t, c % 2) ^ bit, c % 2)
                pairs.append((c * devices + t, c * devices + partner))
        blocks = keep + lax.ppermute(send, (rows_axis, axis), pairs)
        bit *= 2
    return blocks.reshape(rows, width)


def ssd_core(values, b_rows, c_rows, step_size, decay_rate, state):
    length, heads, head_dim = values.shape
    groups = b_rows.shape[1]
    per_group = heads // groups
    blocks = length // SPAN
    lower_mask = (jnp.arange(SPAN)[:, None] >= jnp.arange(SPAN)[None, :])[None]

    def blocked(array):
        return array.reshape((blocks, SPAN) + array.shape[1:])

    def ssd_advance(carry, item):
        value_blk, b_blk, c_blk, step_blk = item
        cums = jnp.cumsum(-step_blk * decay_rate[None, :], axis=0)
        diff = cums.T[:, :, None] - cums.T[:, None, :]
        weight = jnp.where(lower_mask, jnp.exp(jnp.where(lower_mask, diff, 0.0)), 0.0)
        scores = jnp.einsum("tgn,sgn->gts", c_blk, b_blk, precision=HIGH)
        scores = jnp.repeat(scores, per_group, axis=0)
        inputs = step_blk[:, :, None] * value_blk
        inside = jnp.einsum("hts,shp->thp", scores * weight, inputs, precision=HIGH)
        c_head = jnp.repeat(c_blk, per_group, axis=1)
        b_head = jnp.repeat(b_blk, per_group, axis=1)
        carried = jnp.exp(cums)[:, :, None] * jnp.einsum(
            "thn,hpn->thp", c_head, carry, precision=HIGH
        )
        tail = jnp.exp(cums[-1][None, :] - cums)
        fresh = jnp.einsum("shp,shn->hpn", tail[:, :, None] * inputs, b_head, precision=HIGH)
        carry = jnp.exp(cums[-1])[:, None, None] * carry + fresh
        return (carry, inside + carried)

    final, outputs = lax.scan(
        jax.checkpoint(ssd_advance),
        state,
        (blocked(values), blocked(b_rows), blocked(c_rows), blocked(step_size)),
    )
    return (outputs.reshape(length, heads, head_dim), final)


def local_states(values, b_rows, step_size, decay_rate):
    length, heads, head_dim = values.shape
    groups = b_rows.shape[1]
    per_group = heads // groups
    blocks = length // SPAN

    def blocked(array):
        return array.reshape((blocks, SPAN) + array.shape[1:])

    def local_advance(carry, item):
        value_blk, b_blk, step_blk = item
        cums = jnp.cumsum(-step_blk * decay_rate[None, :], axis=0)
        tail = jnp.exp(cums[-1][None, :] - cums)
        b_head = jnp.repeat(b_blk, per_group, axis=1)
        inputs = (tail * step_blk)[:, :, None] * value_blk
        fresh = jnp.einsum("shp,shn->hpn", inputs, b_head, precision=HIGH)
        return (jnp.exp(cums[-1])[:, None, None] * carry + fresh, None)

    start = jnp.zeros((heads, head_dim, STATE), jnp.float32)
    final, unused = lax.scan(
        local_advance, start, (blocked(values), blocked(b_rows), blocked(step_size))
    )
    return final


def local_adjoint(d_mixed, c_rows, step_size, decay_rate):
    length, heads, head_dim = d_mixed.shape
    groups = c_rows.shape[1]
    per_group = heads // groups
    blocks = length // SPAN

    def blocked(array):
        return array.reshape((blocks, SPAN) + array.shape[1:])

    def retreat(carry, item):
        grad_blk, c_blk, step_blk = item
        cums = jnp.cumsum(-step_blk * decay_rate[None, :], axis=0)
        c_head = jnp.repeat(c_blk, per_group, axis=1)
        weighted = jnp.exp(cums)[:, :, None] * grad_blk
        term = jnp.einsum("thp,thn->hpn", weighted, c_head, precision=HIGH)
        return (term + jnp.exp(cums[-1])[:, None, None] * carry, None)

    start = jnp.zeros((heads, head_dim, STATE), jnp.float32)
    final, unused = lax.scan(
        retreat, start, (blocked(d_mixed), blocked(c_rows), blocked(step_size)), reverse=True
    )
    return final


def doubled_rows(x, axis, order):
    devices, position = (lax.axis_size(axis), lax.axis_index(axis))
    for b in order:
        bit = 1 << b
        other = lax.ppermute(x, axis, [(i, i ^ bit) for i in range(devices)])
        low = (position & bit) == 0
        x = jnp.where(low, jnp.concatenate([x, other], 0), jnp.concatenate([other, x], 0))
    rows = x.shape[0] // devices
    x = x.reshape((2,) * len(order) + (rows,) + x.shape[1:])
    axes = [len(order) - 1 - order.index(b) for b in reversed(range(len(order)))]
    x = jnp.transpose(x, axes + list(range(len(order), x.ndim)))
    return x.reshape((devices * rows,) + x.shape[len(order) + 1 :])


def row_block(w, index, size):
    return lax.dynamic_slice_in_dim(w, index * size, size, axis=0)


def per_device(tokens, w_in, w_bc, w_dt, dt_bias, decay_rate, skip_gain, w_out, cotangent):
    devices = lax.axis_size("tp")
    rows, width = tokens.shape
    heads = decay_rate.shape[0]
    inner = w_in.shape[1]
    pair_cols = w_bc.shape[1]
    groups = pair_cols // (2 * STATE)
    out_cols = w_out.shape[0]
    w_all = lax.all_gather(
        jnp.concatenate([w_out.T, w_in, w_bc, w_dt], axis=1), "ctx", axis=0, tiled=True
    )
    bits = devices.bit_length() - 1
    pieces = doubled_rows(
        jnp.concatenate([tokens, cotangent], axis=1), "tp", list(reversed(range(bits)))
    )
    projected = None
    d_flat = None
    for k in range(devices):
        block = w_all[k * width : (k + 1) * width]
        piece = pieces[k * rows : (k + 1) * rows]
        term = jnp.dot(piece[:, :width], block[:, out_cols:], preferred_element_type=jnp.float32)
        projected = term if projected is None else projected + term
        term = jnp.dot(piece[:, width:], block[:, :out_cols], preferred_element_type=jnp.float32)
        d_flat = term if d_flat is None else d_flat + term
    values = projected[:, :inner].astype(jnp.bfloat16)
    pairs = projected[:, inner : inner + pair_cols].astype(jnp.bfloat16)
    pre_step = projected[:, inner + pair_cols :] + dt_bias[None, :]
    step_size = jax.nn.softplus(pre_step)
    value_f = values.astype(jnp.float32).reshape(rows, heads, HEADDIM)
    paired = pairs.astype(jnp.float32).reshape(rows, groups, 2, STATE)
    b_rows = paired[:, :, 0]
    c_rows = paired[:, :, 1]
    end_state = local_states(value_f, b_rows, step_size, decay_rate)
    decay_total = jnp.exp(-jnp.sum(step_size * decay_rate[None, :], axis=0))
    d_mixed = d_flat.reshape(rows, heads, HEADDIM)
    own_adjoint = local_adjoint(d_mixed, c_rows, step_size, decay_rate)
    state_in, adjoint = both_carries(decay_total, end_state, own_adjoint, "ctx")

    def with_state(vals, brows, crows, steps):
        return ssd_core(vals, brows, crows, steps, decay_rate, state_in)

    (core_out, core_end), pullback = jax.vjp(with_state, value_f, b_rows, c_rows, step_size)
    mixed = (
        (core_out + skip_gain[None, :, None] * value_f).reshape(rows, inner).astype(jnp.bfloat16)
    )

    partial_out = lax.dot_general(
        mixed, w_all[:, :out_cols], (((1,), (1,)), ((), ())), preferred_element_type=jnp.float32
    )
    output = scattered_sum(partial_out, "ctx", "tp", width).astype(jnp.bfloat16)
    grads = pullback((d_mixed, adjoint))
    d_values = grads[0] + skip_gain[None, :, None] * d_mixed
    d_pre = grads[3] * jax.nn.sigmoid(pre_step)
    d_pairs = jnp.stack([grads[1], grads[2]], axis=2).reshape(rows, pair_cols)
    d_cat = jnp.concatenate(
        [
            d_values.reshape(rows, inner).astype(jnp.bfloat16),
            d_pairs.astype(jnp.bfloat16),
            d_pre.astype(jnp.bfloat16),
        ],
        axis=1,
    )

    partial_grad = lax.dot_general(
        d_cat, w_all[:, out_cols:], (((1,), (1,)), ((), ())), preferred_element_type=jnp.float32
    )
    grad = scattered_sum(partial_grad, "ctx", "tp", width).astype(jnp.bfloat16)
    return (output, grad)


def solution(mesh):
    placed = (
        P("ctx", "tp"),
        P("ctx", "tp"),
        P("ctx", "tp"),
        P("ctx", "tp"),
        P("tp"),
        P("tp"),
        P("tp"),
        P("tp", "ctx"),
        P("ctx", "tp"),
    )
    return jax.shard_map(
        per_device,
        mesh=mesh,
        in_specs=placed,
        out_specs=(P("ctx", "tp"), P("ctx", "tp")),
        check_vma=False,
    )
```
